32 devices in a mesh: wide: 8 (over z, x), narrow: 4 (over y, core).
Axes of the slice: x: 2, y: 2, z: 4, core: 2. Of those that a mesh axis runs over, the one named last changes fastest.
Arguments:
- stream: bfloat16 [64, 1048576], P(None, ('wide', 'narrow')), may hold values from -96 to 96
- target: bfloat16 [1048576], P(('wide', 'narrow')), may hold values from -400 to 400
- depthwise_taps: float32 [4, 16, 64], replicated, may hold values from -1.5 to 1.5
Outputs:
- coefficients: float32 [256], replicated
- residual: float32 [1048576], P(('wide', 'narrow'))
The draws below stay inside these ranges and needn't reach their ends.
All inputs are finite; a program needn't handle non-finite values.
Results may differ from the reference program's by a relative error of at most 0.0004.
The reference program's roundings to bfloat16 on the way (of `features` and `rounded`) count: a program that leaves them out, or rounds other values in their place, can miss the bound.
Values may be sent and summed in bfloat16 or wider, within the bound.
No kernel may reach another device: no remote copies, remote signals or barrier semaphores. Data moves between devices by JAX's collectives and lax.ppermute only.
A program may use at most 128 MiB of HBM per device.

```python
import math
import jax
import jax.numpy as jnp
from jax import lax

SENSOR_CHANNELS = 64
DILATION_COUNT = 4
FILTER_TAP_COUNT = 16
F = 256
T_DEV = 32768
TIME = 1048576


def sensor_source(key):
    base_key = jax.random.fold_in(key, 7)
    sample_key, key_rough, key_channel, key_mixing, key_noise = jax.random.split(base_key, 5)
    segment_len = T_DEV // 4
    segments = TIME // segment_len
    times = jnp.arange(TIME, dtype=jnp.int32)
    stream_segment = times // segment_len
    samples = jax.random.truncated_normal(sample_key, -4.0, 4.0, (SENSOR_CHANNELS, TIME), jnp.float32)
    roughness = jnp.exp(jax.random.uniform(key_rough, (segments,), jnp.float32, math.log(0.5), math.log(2.0)))
    upward = jnp.exp(math.log(3.0) * times.astype(jnp.float32) / TIME)
    envelope = roughness[stream_segment] * upward
    channel_scale = jnp.exp(jax.random.uniform(key_channel, (SENSOR_CHANNELS,), jnp.float32, math.log(0.4), math.log(4.0)))
    samples = samples * envelope[None, :] * channel_scale[:, None]
    samples = samples.astype(jnp.bfloat16).astype(jnp.float32)
    mixing = jax.random.uniform(key_mixing, (SENSOR_CHANNELS,), jnp.float32, -1.0, 1.0) / (8.0 * channel_scale)
    previous = jnp.pad(samples, ((0, 0), (1, 0)))[:, :TIME]
    noise_term = 0.5 * jax.random.normal(key_noise, (TIME,), jnp.float32) * envelope
    goal = jnp.sum(mixing[:, None] * previous, 0) + noise_term
    return (samples, jnp.clip(goal, -400.0, 400.0))


def draw_stream(key, part):
    samples, goal = sensor_source(key)
    return samples.astype(jnp.bfloat16)


def draw_target(key, part):
    samples, goal = sensor_source(key)
    return goal.astype(jnp.bfloat16)


def bell_draw(own_key, extent, spread, most, kind=jnp.bfloat16):
    values = spread * jax.random.normal(own_key, extent, jnp.float32)
    return jnp.clip(values, min=-most, max=most).astype(kind)


def setup_inputs(seed: int = 0) -> dict:
    keys = jax.random.split(jax.random.key(seed), 4)
    stream = draw_stream(jax.random.fold_in(keys[3], 71), 0)
    target = draw_target(jax.random.fold_in(keys[3], 71), 0)
    depthwise_taps = bell_draw(keys[2], (DILATION_COUNT, FILTER_TAP_COUNT, SENSOR_CHANNELS), FILTER_TAP_COUNT ** -0.5, 1.5, jnp.float32)
    return {"stream": stream, "target": target, "depthwise_taps": depthwise_taps}


ridge_share = 0.05

def dilation_list(top_dilation):
    return (1, top_dilation // 16, top_dilation // 4, top_dilation)

def filter_bank(window, depthwise_taps, top_dilation, history_len, length):
    row_list = []
    for j, d in enumerate(dilation_list(top_dilation)):
        total = jnp.zeros((window.shape[0], length), jnp.float32)
        for k in range(depthwise_taps.shape[1]):
            start_offset = history_len - 1 - k * d
            total = total + depthwise_taps[j, k][:, None] * window[:, start_offset:start_offset + length]
        row_list.append(total.astype(jnp.bfloat16))
    return jnp.concatenate(row_list, 0)

def ridge_solve(system, cross_sum):
    factor = jnp.linalg.cholesky(system)
    middle = lax.linalg.triangular_solve(factor, cross_sum[:, None], left_side=True, lower=True)
    answer = lax.linalg.triangular_solve(factor, middle, left_side=True, lower=True, transpose_a=True)
    return answer[:, 0]

def reference(stream, target, depthwise_taps):
    top_dilation = min(1024, T_DEV // 16)
    history_len = 15 * top_dilation + 1
    padded = jnp.concatenate([jnp.zeros((SENSOR_CHANNELS, history_len), jnp.bfloat16), stream], 1)
    blocks = TIME // T_DEV
    block_numbers = jnp.arange(blocks, dtype=jnp.int32)

    def block_features(block_index):
        start_at = (block_index * T_DEV).astype(jnp.int32)
        window = lax.dynamic_slice_in_dim(padded, start_at, history_len + T_DEV, 1)
        target_block = lax.dynamic_slice_in_dim(target, start_at, T_DEV, 0)
        return (filter_bank(window, depthwise_taps, top_dilation, history_len, T_DEV), target_block)

    def accumulate(running, block_index):
        features, target_block = block_features(block_index)
        gram_sum = lax.dot_general(features.astype(jnp.float32), features.astype(jnp.float32), (((1,), (1,)), ((), ())), preferred_element_type=jnp.float32)
        cross_sum = lax.dot_general(features.astype(jnp.float32), target_block.astype(jnp.float32), (((1,), (0,)), ((), ())), preferred_element_type=jnp.float32)
        return ((running[0] + gram_sum, running[1] + cross_sum), None)
    start_state = (jnp.zeros((F, F), jnp.float32), jnp.zeros((F,), jnp.float32))
    (gram_sum, cross_sum), _ = lax.scan(accumulate, start_state, block_numbers)
    system = gram_sum + ridge_share * TIME * jnp.eye(F, dtype=jnp.float32)
    coefficients = ridge_solve(system, cross_sum)
    rounded = coefficients.astype(jnp.bfloat16)

    def residual_block(block_index):
        features, target_block = block_features(block_index)
        fitted = jnp.dot(rounded.astype(jnp.float32), features.astype(jnp.float32), preferred_element_type=jnp.float32)
        return target_block.astype(jnp.float32) - fitted
    residual = lax.map(residual_block, block_numbers).reshape(TIME)
    return (coefficients, residual)
```

```python
import jax
import jax.numpy as jnp
from jax import lax
from jax.sharding import PartitionSpec as P

ridge_share = 0.05


def shifted(array, axis, by):
    size = lax.axis_size(axis)
    pairs = [(i, i + by) for i in range(size) if 0 <= i + by < size]
    return lax.ppermute(array, axis, pairs)


def dilation_list(top_dilation):
    return (1, top_dilation // 16, top_dilation // 4, top_dilation)


def filter_bank(window, depthwise_taps, top_dilation, history_len, length):
    row_list = []
    for j, d in enumerate(dilation_list(top_dilation)):
        total = jnp.zeros((window.shape[0], length), jnp.float32)
        for k in range(depthwise_taps.shape[1]):
            start_offset = history_len - 1 - k * d
            total = (
                total
                + depthwise_taps[j, k][:, None] * window[:, start_offset : start_offset + length]
            )
        row_list.append(total.astype(jnp.bfloat16))
    return jnp.concatenate(row_list, 0)


def ridge_solve(system, cross_sum):
    factor = jnp.linalg.cholesky(system)
    middle = lax.linalg.triangular_solve(factor, cross_sum[:, None], left_side=True, lower=True)
    answer = lax.linalg.triangular_solve(
        factor, middle, left_side=True, lower=True, transpose_a=True
    )
    return answer[:, 0]


def butterfly_sum(x, axes):
    size = 1
    for name in axes:
        size *= lax.axis_size(name)
    if size & (size - 1):
        return lax.psum(x, axes)
    step = 1
    while step < size:
        x = x + lax.ppermute(x, axes, [(i, i ^ step) for i in range(size)])
        step *= 2
    return x


def reduce_system(gram_sum, cross_sum, axes):
    n = gram_sum.shape[0]
    h = n // 2
    rows = lax.broadcasted_iota(jnp.int32, (h, h), 0)
    cols = lax.broadcasted_iota(jnp.int32, (h, h), 1)
    lead, off, trail = gram_sum[:h, :h], gram_sum[:h, h:], gram_sum[h:, h:]
    folded = jnp.where(rows <= cols, lead, trail)
    extra = jnp.stack([cross_sum, jnp.concatenate([jnp.diagonal(trail), jnp.zeros((n - h,), jnp.float32)])])
    packed = jnp.concatenate([jnp.concatenate([folded, off], 1), extra], 0)
    packed = butterfly_sum(packed, axes)
    folded, off = packed[:h, :h], packed[:h, h:]
    upper = jnp.where(rows <= cols, folded, 0.0)
    lead = upper + jnp.where(rows < cols, folded, 0.0).T
    strict = jnp.where(rows > cols, folded, 0.0)
    trail = strict + strict.T + jnp.diag(packed[h + 1, :h])
    gram_sum = jnp.concatenate(
        [jnp.concatenate([lead, off], 1), jnp.concatenate([off.T, trail], 1)], 0
    )
    return gram_sum, packed[h]


def local(stream, target, depthwise_taps):
    length = stream.shape[1]
    top_dilation = min(1024, length // 16)
    history_len = 15 * top_dilation + 1
    tail_end = stream[:, length - history_len :]
    previous = shifted(tail_end, ("wide", "narrow"), 1)
    window = jnp.concatenate([previous, stream], 1)
    features = filter_bank(window, depthwise_taps, top_dilation, history_len, length)
    gram_sum = lax.dot_general(
        features, features, (((1,), (1,)), ((), ())), preferred_element_type=jnp.float32
    )
    cross_sum = lax.dot_general(
        features, target, (((1,), (0,)), ((), ())), preferred_element_type=jnp.float32
    )
    gram_sum, cross_sum = reduce_system(gram_sum, cross_sum, ("wide", "narrow"))
    total_rows = length * lax.axis_size("wide") * lax.axis_size("narrow")
    system = gram_sum + ridge_share * total_rows * jnp.eye(gram_sum.shape[0], dtype=jnp.float32)
    coefficients = ridge_solve(system, cross_sum)
    rounded = coefficients.astype(jnp.bfloat16)
    fitted = jnp.dot(rounded, features, preferred_element_type=jnp.float32)
    return (coefficients, target.astype(jnp.float32) - fitted)


def solution(mesh):
    in_specs = (P(None, ("wide", "narrow")), P(("wide", "narrow")), P())
    out_specs = (P(), P(("wide", "narrow")))
    return jax.shard_map(local, mesh=mesh, in_specs=in_specs, out_specs=out_specs, check_vma=False)
```

```python
import functools

import jax
import jax.numpy as jnp
from jax import lax
from jax.sharding import PartitionSpec as P
from jax.experimental import pallas as pl
from jax.experimental.pallas import tpu as pltpu

ridge_share = 0.05


def shifted(array, axis, by):
    size = lax.axis_size(axis)
    pairs = [(i, i + by) for i in range(size) if 0 <= i + by < size]
    return lax.ppermute(array, axis, pairs)


def dilation_list(top_dilation):
    return (1, top_dilation // 16, top_dilation // 4, top_dilation)


def filter_bank(window, depthwise_taps, top_dilation, history_len, length):
    row_list = []
    for j, d in enumerate(dilation_list(top_dilation)):
        total = jnp.zeros((window.shape[0], length), jnp.float32)
        for k in range(depthwise_taps.shape[1]):
            start_offset = history_len - 1 - k * d
            total = (
                total
                + depthwise_taps[j, k][:, None] * window[:, start_offset : start_offset + length]
            )
        row_list.append(total.astype(jnp.bfloat16))
    return jnp.concatenate(row_list, 0)


TIME_BLOCK = 2048
CHUNK = 256


def feature_kernel(dilations, span, taps_per_filter, chunk, w_ref, taps_ref, tgt_ref, f_ref, g_ref, c_ref):
    block = pl.program_id(0)
    block_len = f_ref.shape[1]
    channels = w_ref.shape[0]

    @pl.when(block == 0)
    def _():
        g_ref[...] = jnp.zeros_like(g_ref)
        c_ref[...] = jnp.zeros_like(c_ref)

    for j, d in enumerate(dilations):
        def chunk_body(i, carry, j=j, d=d):
            start = pl.multiple_of(block * block_len + i * chunk, 128)
            slabs = {}
            acc = None
            for k in range(taps_per_filter):
                offset = span - k * d
                r = offset % 128
                a = offset - r
                if r == 0:
                    x = w_ref[:, pl.ds(pl.multiple_of(start + a, 128), chunk)].astype(jnp.float32)
                else:
                    if a not in slabs:
                        slabs[a] = w_ref[:, pl.ds(pl.multiple_of(start + a, 128), chunk + 128)].astype(jnp.float32)
                    x = slabs[a][:, r:r + chunk]
                w = jnp.tile(taps_ref[j * taps_per_filter + k], (1, chunk // 128))
                acc = w * x if acc is None else acc + w * x
            f_ref[j * channels:(j + 1) * channels, pl.ds(pl.multiple_of(i * chunk, 128), chunk)] = acc.astype(f_ref.dtype)
            return carry

        lax.fori_loop(0, block_len // chunk, chunk_body, 0)

    feats = f_ref[...]
    g_ref[...] += lax.dot_general(feats, feats, (((1,), (1,)), ((), ())), preferred_element_type=jnp.float32)
    c_ref[...] += lax.dot_general(tgt_ref[...], feats, (((1,), (1,)), ((), ())), preferred_element_type=jnp.float32)


def features_and_sums(window, depthwise_taps, target, top_dilation, length, interpret=False):
    channels = window.shape[0]
    dilations = dilation_list(top_dilation)
    n_filters, taps_per_filter = len(dilations), depthwise_taps.shape[1]
    span = (taps_per_filter - 1) * top_dilation
    rows = n_filters * channels
    block_len = min(TIME_BLOCK, length)
    taps = jnp.broadcast_to(
        depthwise_taps.reshape(n_filters * taps_per_filter, channels, 1),
        (n_filters * taps_per_filter, channels, 128),
    )
    kernel = functools.partial(feature_kernel, dilations, span, taps_per_filter, min(CHUNK, block_len))
    return pl.pallas_call(
        kernel,
        grid=(length // block_len,),
        in_specs=[
            pl.BlockSpec(memory_space=pltpu.VMEM),
            pl.BlockSpec(memory_space=pltpu.VMEM),
            pl.BlockSpec((1, block_len), lambda b: (0, b)),
        ],
        out_specs=[
            pl.BlockSpec((rows, block_len), lambda b: (0, b)),
            pl.BlockSpec((rows, rows), lambda b: (0, 0)),
            pl.BlockSpec((1, rows), lambda b: (0, 0)),
        ],
        out_shape=[
            jax.ShapeDtypeStruct((rows, length), jnp.bfloat16),
            jax.ShapeDtypeStruct((rows, rows), jnp.float32),
            jax.ShapeDtypeStruct((1, rows), jnp.float32),
        ],
        compiler_params=pltpu.CompilerParams(
            dimension_semantics=("arbitrary",), vmem_limit_bytes=48 * 1024 * 1024
        ),
        interpret=interpret,
    )(window, taps, target.reshape(1, length))


def ridge_solve(system, cross_sum):
    factor = jnp.linalg.cholesky(system)
    middle = lax.linalg.triangular_solve(factor, cross_sum[:, None], left_side=True, lower=True)
    answer = lax.linalg.triangular_solve(
        factor, middle, left_side=True, lower=True, transpose_a=True
    )
    return answer[:, 0]


def butterfly_sum(x, axes):
    size = 1
    for name in axes:
        size *= lax.axis_size(name)
    if size & (size - 1):
        return lax.psum(x, axes)
    step = 1
    while step < size:
        x = x + lax.ppermute(x, axes, [(i, i ^ step) for i in range(size)])
        step *= 2
    return x


def reduce_system(gram_sum, cross_sum, axes):
    n = gram_sum.shape[0]
    h = n // 2
    rows = lax.broadcasted_iota(jnp.int32, (h, h), 0)
    cols = lax.broadcasted_iota(jnp.int32, (h, h), 1)
    lead, off, trail = gram_sum[:h, :h], gram_sum[:h, h:], gram_sum[h:, h:]
    folded = jnp.where(rows <= cols, lead, trail)
    extra = jnp.stack([cross_sum, jnp.concatenate([jnp.diagonal(trail), jnp.zeros((n - h,), jnp.float32)])])
    packed = jnp.concatenate([jnp.concatenate([folded, off], 1), extra], 0)
    packed = butterfly_sum(packed, axes)
    folded, off = packed[:h, :h], packed[:h, h:]
    upper = jnp.where(rows <= cols, folded, 0.0)
    lead = upper + jnp.where(rows < cols, folded, 0.0).T
    strict = jnp.where(rows > cols, folded, 0.0)
    trail = strict + strict.T + jnp.diag(packed[h + 1, :h])
    gram_sum = jnp.concatenate(
        [jnp.concatenate([lead, off], 1), jnp.concatenate([off.T, trail], 1)], 0
    )
    return gram_sum, packed[h]


def local(stream, target, depthwise_taps):
    length = stream.shape[1]
    top_dilation = min(1024, length // 16)
    history_len = 15 * top_dilation + 1
    tail_end = stream[:, length - history_len :]
    previous = shifted(tail_end, ("wide", "narrow"), 1)
    window = jnp.concatenate([previous, stream], 1)[:, : history_len - 1 + length]
    features, gram_sum, cross_sum = features_and_sums(window, depthwise_taps, target, top_dilation, length)
    cross_sum = cross_sum[0]
    gram_sum, cross_sum = reduce_system(gram_sum, cross_sum, ("wide", "narrow"))
    total_rows = length * lax.axis_size("wide") * lax.axis_size("narrow")
    system = gram_sum + ridge_share * total_rows * jnp.eye(gram_sum.shape[0], dtype=jnp.float32)
    coefficients = ridge_solve(system, cross_sum)
    rounded = coefficients.astype(jnp.bfloat16)
    fitted = jnp.dot(rounded, features, preferred_element_type=jnp.float32)
    return (coefficients, target.astype(jnp.float32) - fitted)


def solution(mesh):
    in_specs = (P(None, ("wide", "narrow")), P(("wide", "narrow")), P())
    out_specs = (P(), P(("wide", "narrow")))
    return jax.shard_map(local, mesh=mesh, in_specs=in_specs, out_specs=out_specs, check_vma=False)
```

```python
import functools

import jax
import jax.numpy as jnp
from jax import lax
from jax.sharding import PartitionSpec as P
from jax.experimental import pallas as pl
from jax.experimental.pallas import tpu as pltpu

ridge_share = 0.05


def shifted(array, axis, by):
    size = lax.axis_size(axis)
    pairs = [(i, i + by) for i in range(size) if 0 <= i + by < size]
    return lax.ppermute(array, axis, pairs)


def dilation_list(top_dilation):
    return (1, top_dilation // 16, top_dilation // 4, top_dilation)


def filter_bank(window, depthwise_taps, top_dilation, history_len, length):
    row_list = []
    for j, d in enumerate(dilation_list(top_dilation)):
        total = jnp.zeros((window.shape[0], length), jnp.float32)
        for k in range(depthwise_taps.shape[1]):
            start_offset = history_len - 1 - k * d
            total = (
                total
                + depthwise_taps[j, k][:, None] * window[:, start_offset : start_offset + length]
            )
        row_list.append(total.astype(jnp.bfloat16))
    return jnp.concatenate(row_list, 0)


TIME_BLOCK = 2048
CHUNK = 256


def feature_kernel(dilations, span, taps_per_filter, chunk, w_ref, taps_ref, tgt_ref, f_ref, g_ref, c_ref):
    block = pl.program_id(0)
    block_len = f_ref.shape[1]
    channels = w_ref.shape[0]

    @pl.when(block == 0)
    def _():
        g_ref[...] = jnp.zeros_like(g_ref)
        c_ref[...] = jnp.zeros_like(c_ref)

    for j, d in enumerate(dilations):
        def chunk_body(i, carry, j=j, d=d):
            start = pl.multiple_of(block * block_len + i * chunk, 128)
            slabs = {}
            acc = None
            for k in range(taps_per_filter):
                offset = span - k * d
                r = offset % 128
                a = offset - r
                if r == 0:
                    x = w_ref[:, pl.ds(pl.multiple_of(start + a, 128), chunk)].astype(jnp.float32)
                else:
                    if a not in slabs:
                        slabs[a] = w_ref[:, pl.ds(pl.multiple_of(start + a, 128), chunk + 128)].astype(jnp.float32)
                    x = slabs[a][:, r:r + chunk]
                w = jnp.tile(taps_ref[j * taps_per_filter + k], (1, chunk // 128))
                acc = w * x if acc is None else acc + w * x
            f_ref[j * channels:(j + 1) * channels, pl.ds(pl.multiple_of(i * chunk, 128), chunk)] = acc.astype(f_ref.dtype)
            return carry

        lax.fori_loop(0, block_len // chunk, chunk_body, 0)

    feats = f_ref[...]
    g_ref[...] += lax.dot_general(feats, feats, (((1,), (1,)), ((), ())), preferred_element_type=jnp.float32)
    c_ref[...] += lax.dot_general(tgt_ref[...], feats, (((1,), (1,)), ((), ())), preferred_element_type=jnp.float32)


def features_and_sums(window, depthwise_taps, target, top_dilation, length, interpret=False):
    channels = window.shape[0]
    dilations = dilation_list(top_dilation)
    n_filters, taps_per_filter = len(dilations), depthwise_taps.shape[1]
    span = (taps_per_filter - 1) * top_dilation
    rows = n_filters * channels
    block_len = min(TIME_BLOCK, length)
    taps = jnp.broadcast_to(
        depthwise_taps.reshape(n_filters * taps_per_filter, channels, 1),
        (n_filters * taps_per_filter, channels, 128),
    )
    kernel = functools.partial(feature_kernel, dilations, span, taps_per_filter, min(CHUNK, block_len))
    return pl.pallas_call(
        kernel,
        grid=(length // block_len,),
        in_specs=[
            pl.BlockSpec(memory_space=pltpu.VMEM),
            pl.BlockSpec(memory_space=pltpu.VMEM),
            pl.BlockSpec((1, block_len), lambda b: (0, b)),
        ],
        out_specs=[
            pl.BlockSpec((rows, block_len), lambda b: (0, b)),
            pl.BlockSpec((rows, rows), lambda b: (0, 0)),
            pl.BlockSpec((1, rows), lambda b: (0, 0)),
        ],
        out_shape=[
            jax.ShapeDtypeStruct((rows, length), jnp.bfloat16),
            jax.ShapeDtypeStruct((rows, rows), jnp.float32),
            jax.ShapeDtypeStruct((1, rows), jnp.float32),
        ],
        compiler_params=pltpu.CompilerParams(
            dimension_semantics=("arbitrary",), vmem_limit_bytes=48 * 1024 * 1024
        ),
        interpret=interpret,
    )(window, taps, target.reshape(1, length))


def solve_kernel(system_ref, c_ref, x_ref, a_ref, lt_ref):
    n = a_ref.shape[0]
    a_ref[...] = system_ref[...]
    lanes = lax.broadcasted_iota(jnp.int32, (1, n), 1)

    def pick(vec, at):
        return jnp.sum(jnp.where(at, vec, 0.0), axis=1, keepdims=True)

    def factor_step(j, carry):
        rhs, forward, diag = carry
        at = lanes == j
        row = a_ref[pl.ds(j, 1), :]
        root = jnp.sqrt(pick(row, at))
        col_j = jnp.where(lanes >= j, row / root, 0.0)
        lt_ref[pl.ds(j, 1), :] = col_j
        yj = pick(rhs, at) / root
        rhs = rhs - yj * col_j
        forward = jnp.where(at, yj, forward)
        diag = jnp.where(at, root, diag)
        column = jnp.transpose(jnp.broadcast_to(col_j, (8, n)))[:, 0:1]
        a_ref[...] = a_ref[...] - column * col_j
        return rhs, forward, diag

    zeros = jnp.zeros((1, n), jnp.float32)
    _, forward, diag = lax.fori_loop(0, n, factor_step, (c_ref[...], zeros, zeros))

    def back_step(t, x):
        j = n - 1 - t
        at = lanes == j
        partial = jnp.sum(lt_ref[pl.ds(j, 1), :] * x, axis=1, keepdims=True)
        return jnp.where(at, (pick(forward, at) - partial) / pick(diag, at), x)

    x_ref[...] = lax.fori_loop(0, n, back_step, zeros)


def ridge_solve_kernel(system, cross_sum, interpret=False):
    n = system.shape[0]
    return pl.pallas_call(
        solve_kernel,
        in_specs=[pl.BlockSpec(memory_space=pltpu.VMEM), pl.BlockSpec(memory_space=pltpu.VMEM)],
        out_specs=pl.BlockSpec(memory_space=pltpu.VMEM),
        out_shape=jax.ShapeDtypeStruct((1, n), jnp.float32),
        scratch_shapes=[pltpu.VMEM((n, n), jnp.float32), pltpu.VMEM((n, n), jnp.float32)],
        interpret=interpret,
    )(system, cross_sum.reshape(1, n))[0]


def ridge_solve(system, cross_sum):
    factor = jnp.linalg.cholesky(system)
    middle = lax.linalg.triangular_solve(factor, cross_sum[:, None], left_side=True, lower=True)
    answer = lax.linalg.triangular_solve(
        factor, middle, left_side=True, lower=True, transpose_a=True
    )
    return answer[:, 0]


def butterfly_sum(x, axes):
    size = 1
    for name in axes:
        size *= lax.axis_size(name)
    if size & (size - 1):
        return lax.psum(x, axes)
    step = 1
    while step < size:
        x = x + lax.ppermute(x, axes, [(i, i ^ step) for i in range(size)])
        step *= 2
    return x


def reduce_system(gram_sum, cross_sum, axes):
    n = gram_sum.shape[0]
    h = n // 2
    rows = lax.broadcasted_iota(jnp.int32, (h, h), 0)
    cols = lax.broadcasted_iota(jnp.int32, (h, h), 1)
    lead, off, trail = gram_sum[:h, :h], gram_sum[:h, h:], gram_sum[h:, h:]
    folded = jnp.where(rows <= cols, lead, trail)
    extra = jnp.stack([cross_sum, jnp.concatenate([jnp.diagonal(trail), jnp.zeros((n - h,), jnp.float32)])])
    packed = jnp.concatenate([jnp.concatenate([folded, off], 1), extra], 0)
    packed = butterfly_sum(packed, axes)
    folded, off = packed[:h, :h], packed[:h, h:]
    upper = jnp.where(rows <= cols, folded, 0.0)
    lead = upper + jnp.where(rows < cols, folded, 0.0).T
    strict = jnp.where(rows > cols, folded, 0.0)
    trail = strict + strict.T + jnp.diag(packed[h + 1, :h])
    gram_sum = jnp.concatenate(
        [jnp.concatenate([lead, off], 1), jnp.concatenate([off.T, trail], 1)], 0
    )
    return gram_sum, packed[h]


def local(stream, target, depthwise_taps):
    length = stream.shape[1]
    top_dilation = min(1024, length // 16)
    history_len = 15 * top_dilation + 1
    tail_end = stream[:, length - history_len :]
    previous = shifted(tail_end, ("wide", "narrow"), 1)
    window = jnp.concatenate([previous, stream], 1)[:, : history_len - 1 + length]
    features, gram_sum, cross_sum = features_and_sums(window, depthwise_taps, target, top_dilation, length)
    cross_sum = cross_sum[0]
    gram_sum, cross_sum = reduce_system(gram_sum, cross_sum, ("wide", "narrow"))
    total_rows = length * lax.axis_size("wide") * lax.axis_size("narrow")
    system = gram_sum + ridge_share * total_rows * jnp.eye(gram_sum.shape[0], dtype=jnp.float32)
    coefficients = ridge_solve_kernel(system, cross_sum)
    rounded = coefficients.astype(jnp.bfloat16)
    fitted = jnp.dot(rounded, features, preferred_element_type=jnp.float32)
    return (coefficients, target.astype(jnp.float32) - fitted)


def solution(mesh):
    in_specs = (P(None, ("wide", "narrow")), P(("wide", "narrow")), P())
    out_specs = (P(), P(("wide", "narrow")))
    return jax.shard_map(local, mesh=mesh, in_specs=in_specs, out_specs=out_specs, check_vma=False)
```

```python
import functools

import jax
import jax.numpy as jnp
from jax import lax
from jax.sharding import PartitionSpec as P
from jax.experimental import pallas as pl
from jax.experimental.pallas import tpu as pltpu

ridge_share = 0.05


def shifted(array, axis, by):
    size = lax.axis_size(axis)
    pairs = [(i, i + by) for i in range(size) if 0 <= i + by < size]
    return lax.ppermute(array, axis, pairs)


def dilation_list(top_dilation):
    return (1, top_dilation // 16, top_dilation // 4, top_dilation)


def filter_bank(window, depthwise_taps, top_dilation, history_len, length):
    row_list = []
    for j, d in enumerate(dilation_list(top_dilation)):
        total = jnp.zeros((window.shape[0], length), jnp.float32)
        for k in range(depthwise_taps.shape[1]):
            start_offset = history_len - 1 - k * d
            total = (
                total
                + depthwise_taps[j, k][:, None] * window[:, start_offset : start_offset + length]
            )
        row_list.append(total.astype(jnp.bfloat16))
    return jnp.concatenate(row_list, 0)


TIME_BLOCK = 2048
CHUNK = 256


def feature_kernel(dilations, span, taps_per_filter, chunk, w_ref, taps_ref, tgt_ref, f_ref, g_ref, c_ref, wf_ref):
    block = pl.program_id(0)
    block_len = f_ref.shape[1]
    channels = w_ref.shape[0]

    @pl.when(block == 0)
    def _():
        g_ref[...] = jnp.zeros_like(g_ref)
        c_ref[...] = jnp.zeros_like(c_ref)

        def widen(i, carry):
            lanes = pl.ds(pl.multiple_of(i * 128, 128), 128)
            wf_ref[:, lanes] = w_ref[:, lanes].astype(jnp.float32)
            return carry

        lax.fori_loop(0, w_ref.shape[1] // 128, widen, 0)

    for j, d in enumerate(dilations):
        def chunk_body(i, carry, j=j, d=d):
            start = pl.multiple_of(block * block_len + i * chunk, 128)
            slabs = {}
            acc = None
            for k in range(taps_per_filter):
                offset = span - k * d
                r = offset % 128
                a = offset - r
                if r == 0:
                    x = wf_ref[:, pl.ds(pl.multiple_of(start + a, 128), chunk)]
                else:
                    if a not in slabs:
                        slabs[a] = wf_ref[:, pl.ds(pl.multiple_of(start + a, 128), chunk + 128)]
                    x = slabs[a][:, r:r + chunk]
                w = jnp.tile(taps_ref[j * taps_per_filter + k], (1, chunk // 128))
                acc = w * x if acc is None else acc + w * x
            f_ref[j * channels:(j + 1) * channels, pl.ds(pl.multiple_of(i * chunk, 128), chunk)] = acc.astype(f_ref.dtype)
            return carry

        lax.fori_loop(0, block_len // chunk, chunk_body, 0)

    feats = f_ref[...]
    g_ref[...] += lax.dot_general(feats, feats, (((1,), (1,)), ((), ())), preferred_element_type=jnp.float32)
    c_ref[...] += lax.dot_general(tgt_ref[...], feats, (((1,), (1,)), ((), ())), preferred_element_type=jnp.float32)


def features_and_sums(window, depthwise_taps, target, top_dilation, length, interpret=False):
    channels = window.shape[0]
    dilations = dilation_list(top_dilation)
    n_filters, taps_per_filter = len(dilations), depthwise_taps.shape[1]
    span = (taps_per_filter - 1) * top_dilation
    rows = n_filters * channels
    block_len = min(TIME_BLOCK, length)
    taps = jnp.broadcast_to(
        depthwise_taps.reshape(n_filters * taps_per_filter, channels, 1),
        (n_filters * taps_per_filter, channels, 128),
    )
    kernel = functools.partial(feature_kernel, dilations, span, taps_per_filter, min(CHUNK, block_len))
    return pl.pallas_call(
        kernel,
        grid=(length // block_len,),
        in_specs=[
            pl.BlockSpec(memory_space=pltpu.VMEM),
            pl.BlockSpec(memory_space=pltpu.VMEM),
            pl.BlockSpec((1, block_len), lambda b: (0, b)),
        ],
        out_specs=[
            pl.BlockSpec((rows, block_len), lambda b: (0, b)),
            pl.BlockSpec((rows, rows), lambda b: (0, 0)),
            pl.BlockSpec((1, rows), lambda b: (0, 0)),
        ],
        out_shape=[
            jax.ShapeDtypeStruct((rows, length), jnp.bfloat16),
            jax.ShapeDtypeStruct((rows, rows), jnp.float32),
            jax.ShapeDtypeStruct((1, rows), jnp.float32),
        ],
        scratch_shapes=[pltpu.VMEM(window.shape, jnp.float32)],
        compiler_params=pltpu.CompilerParams(
            dimension_semantics=("arbitrary",), vmem_limit_bytes=48 * 1024 * 1024
        ),
        interpret=interpret,
    )(window, taps, target.reshape(1, length))


def solve_kernel(system_ref, c_ref, x_ref, a_ref, lt_ref):
    n = a_ref.shape[0]
    a_ref[...] = system_ref[...]
    lanes = lax.broadcasted_iota(jnp.int32, (1, n), 1)

    def pick(vec, at):
        return jnp.sum(jnp.where(at, vec, 0.0), axis=1, keepdims=True)

    def factor_step(j, carry):
        rhs, forward, diag = carry
        at = lanes == j
        row = a_ref[pl.ds(j, 1), :]
        root = jnp.sqrt(pick(row, at))
        col_j = jnp.where(lanes >= j, row / root, 0.0)
        lt_ref[pl.ds(j, 1), :] = col_j
        yj = pick(rhs, at) / root
        rhs = rhs - yj * col_j
        forward = jnp.where(at, yj, forward)
        diag = jnp.where(at, root, diag)
        column = jnp.transpose(jnp.broadcast_to(col_j, (8, n)))[:, 0:1]
        a_ref[...] = a_ref[...] - column * col_j
        return rhs, forward, diag

    zeros = jnp.zeros((1, n), jnp.float32)
    _, forward, diag = lax.fori_loop(0, n, factor_step, (c_ref[...], zeros, zeros))

    def back_step(t, x):
        j = n - 1 - t
        at = lanes == j
        partial = jnp.sum(lt_ref[pl.ds(j, 1), :] * x, axis=1, keepdims=True)
        return jnp.where(at, (pick(forward, at) - partial) / pick(diag, at), x)

    x_ref[...] = lax.fori_loop(0, n, back_step, zeros)


def ridge_solve_kernel(system, cross_sum, interpret=False):
    n = system.shape[0]
    return pl.pallas_call(
        solve_kernel,
        in_specs=[pl.BlockSpec(memory_space=pltpu.VMEM), pl.BlockSpec(memory_space=pltpu.VMEM)],
        out_specs=pl.BlockSpec(memory_space=pltpu.VMEM),
        out_shape=jax.ShapeDtypeStruct((1, n), jnp.float32),
        scratch_shapes=[pltpu.VMEM((n, n), jnp.float32), pltpu.VMEM((n, n), jnp.float32)],
        interpret=interpret,
    )(system, cross_sum.reshape(1, n))[0]


def ridge_solve(system, cross_sum):
    factor = jnp.linalg.cholesky(system)
    middle = lax.linalg.triangular_solve(factor, cross_sum[:, None], left_side=True, lower=True)
    answer = lax.linalg.triangular_solve(
        factor, middle, left_side=True, lower=True, transpose_a=True
    )
    return answer[:, 0]


def butterfly_sum(x, axes):
    size = 1
    for name in axes:
        size *= lax.axis_size(name)
    if size & (size - 1):
        return lax.psum(x, axes)
    step = 1
    while step < size:
        x = x + lax.ppermute(x, axes, [(i, i ^ step) for i in range(size)])
        step *= 2
    return x


def reduce_system(gram_sum, cross_sum, axes):
    n = gram_sum.shape[0]
    h = n // 2
    rows = lax.broadcasted_iota(jnp.int32, (h, h), 0)
    cols = lax.broadcasted_iota(jnp.int32, (h, h), 1)
    lead, off, trail = gram_sum[:h, :h], gram_sum[:h, h:], gram_sum[h:, h:]
    folded = jnp.where(rows <= cols, lead, trail)
    extra = jnp.stack([cross_sum, jnp.concatenate([jnp.diagonal(trail), jnp.zeros((n - h,), jnp.float32)])])
    packed = jnp.concatenate([jnp.concatenate([folded, off], 1), extra], 0)
    packed = butterfly_sum(packed, axes)
    folded, off = packed[:h, :h], packed[:h, h:]
    upper = jnp.where(rows <= cols, folded, 0.0)
    lead = upper + jnp.where(rows < cols, folded, 0.0).T
    strict = jnp.where(rows > cols, folded, 0.0)
    trail = strict + strict.T + jnp.diag(packed[h + 1, :h])
    gram_sum = jnp.concatenate(
        [jnp.concatenate([lead, off], 1), jnp.concatenate([off.T, trail], 1)], 0
    )
    return gram_sum, packed[h]


def local(stream, target, depthwise_taps):
    length = stream.shape[1]
    top_dilation = min(1024, length // 16)
    history_len = 15 * top_dilation + 1
    tail_end = stream[:, length - history_len :]
    previous = shifted(tail_end, ("wide", "narrow"), 1)
    window = jnp.concatenate([previous, stream], 1)[:, : history_len - 1 + length]
    features, gram_sum, cross_sum = features_and_sums(window, depthwise_taps, target, top_dilation, length)
    cross_sum = cross_sum[0]
    gram_sum, cross_sum = reduce_system(gram_sum, cross_sum, ("wide", "narrow"))
    total_rows = length * lax.axis_size("wide") * lax.axis_size("narrow")
    system = gram_sum + ridge_share * total_rows * jnp.eye(gram_sum.shape[0], dtype=jnp.float32)
    coefficients = ridge_solve(system, cross_sum)
    rounded = coefficients.astype(jnp.bfloat16)
    fitted = jnp.dot(rounded, features, preferred_element_type=jnp.float32)
    return (coefficients, target.astype(jnp.float32) - fitted)


def solution(mesh):
    in_specs = (P(None, ("wide", "narrow")), P(("wide", "narrow")), P())
    out_specs = (P(), P(("wide", "narrow")))
    return jax.shard_map(local, mesh=mesh, in_specs=in_specs, out_specs=out_specs, check_vma=False)
```

```python
import functools

import jax
import jax.numpy as jnp
from jax import lax
from jax.sharding import PartitionSpec as P
from jax.experimental import pallas as pl
from jax.experimental.pallas import tpu as pltpu

ridge_share = 0.05


def shifted(array, axis, by):
    size = lax.axis_size(axis)
    pairs = [(i, i + by) for i in range(size) if 0 <= i + by < size]
    return lax.ppermute(array, axis, pairs)


def dilation_list(top_dilation):
    return (1, top_dilation // 16, top_dilation // 4, top_dilation)


def filter_bank(window, depthwise_taps, top_dilation, history_len, length):
    row_list = []
    for j, d in enumerate(dilation_list(top_dilation)):
        total = jnp.zeros((window.shape[0], length), jnp.float32)
        for k in range(depthwise_taps.shape[1]):
            start_offset = history_len - 1 - k * d
            total = (
                total
                + depthwise_taps[j, k][:, None] * window[:, start_offset : start_offset + length]
            )
        row_list.append(total.astype(jnp.bfloat16))
    return jnp.concatenate(row_list, 0)


TIME_BLOCK = 2048
ROW_GROUP = 16
NARROW_CHUNK = 1024
WIDE_CHUNK = 1024


def feature_kernel(dilations, span, taps_per_filter, w_ref, taps_ref, tgt_ref, f_ref, g_ref, c_ref):
    block = pl.program_id(0)
    block_len = f_ref.shape[1]
    channels = w_ref.shape[0]
    group = ROW_GROUP

    @pl.when(block == 0)
    def _():
        g_ref[...] = jnp.zeros_like(g_ref)
        c_ref[...] = jnp.zeros_like(c_ref)

    for j, d in enumerate(dilations):
        chunk = min(block_len, NARROW_CHUNK if d % 64 else WIDE_CHUNK)
        for g in range(channels // group):
            rows = pl.ds(g * group, group)

            def chunk_body(i, carry, j=j, d=d, rows=rows, g=g, chunk=chunk):
                start = pl.multiple_of(block * block_len + i * chunk, 128)
                slabs = {}
                acc = None
                for k in range(taps_per_filter):
                    offset = span - k * d
                    r = offset % 128
                    a = offset - r
                    if r == 0:
                        x = w_ref[rows, pl.ds(pl.multiple_of(start + a, 128), chunk)].astype(jnp.float32)
                    else:
                        if a not in slabs:
                            slabs[a] = w_ref[rows, pl.ds(pl.multiple_of(start + a, 128), chunk + 128)].astype(jnp.float32)
                        x = slabs[a][:, r:r + chunk]
                    w = jnp.tile(taps_ref[j * taps_per_filter + k, rows, :], (1, chunk // 128))
                    acc = w * x if acc is None else acc + w * x
                out_rows = pl.ds(j * channels + g * group, group)
                f_ref[out_rows, pl.ds(pl.multiple_of(i * chunk, 128), chunk)] = acc.astype(f_ref.dtype)
                return carry

            lax.fori_loop(0, block_len // chunk, chunk_body, 0)

    feats = f_ref[...]
    g_ref[...] += lax.dot_general(feats, feats, (((1,), (1,)), ((), ())), preferred_element_type=jnp.float32)
    c_ref[...] += lax.dot_general(tgt_ref[...], feats, (((1,), (1,)), ((), ())), preferred_element_type=jnp.float32)


def features_and_sums(window, depthwise_taps, target, top_dilation, length, interpret=False):
    channels = window.shape[0]
    dilations = dilation_list(top_dilation)
    n_filters, taps_per_filter = len(dilations), depthwise_taps.shape[1]
    span = (taps_per_filter - 1) * top_dilation
    rows = n_filters * channels
    block_len = min(TIME_BLOCK, length)
    taps = jnp.broadcast_to(
        depthwise_taps.reshape(n_filters * taps_per_filter, channels, 1),
        (n_filters * taps_per_filter, channels, 128),
    )
    kernel = functools.partial(feature_kernel, dilations, span, taps_per_filter)
    return pl.pallas_call(
        kernel,
        grid=(length // block_len,),
        in_specs=[
            pl.BlockSpec(memory_space=pltpu.VMEM),
            pl.BlockSpec(memory_space=pltpu.VMEM),
            pl.BlockSpec((1, block_len), lambda b: (0, b)),
        ],
        out_specs=[
            pl.BlockSpec((rows, block_len), lambda b: (0, b)),
            pl.BlockSpec((rows, rows), lambda b: (0, 0)),
            pl.BlockSpec((1, rows), lambda b: (0, 0)),
        ],
        out_shape=[
            jax.ShapeDtypeStruct((rows, length), jnp.bfloat16),
            jax.ShapeDtypeStruct((rows, rows), jnp.float32),
            jax.ShapeDtypeStruct((1, rows), jnp.float32),
        ],
        compiler_params=pltpu.CompilerParams(
            dimension_semantics=("arbitrary",), vmem_limit_bytes=48 * 1024 * 1024
        ),
        interpret=interpret,
    )(window, taps, target.reshape(1, length))


def solve_kernel(system_ref, c_ref, x_ref, a_ref, lt_ref):
    n = a_ref.shape[0]
    a_ref[...] = system_ref[...]
    lanes = lax.broadcasted_iota(jnp.int32, (1, n), 1)
    sublanes = lax.broadcasted_iota(jnp.int32, (n, 1), 0)

    def pick(vec, at):
        return jnp.sum(jnp.where(at, vec, 0.0), axis=1, keepdims=True)

    def factor_step(j, carry):
        rhs, forward, diag = carry
        at = lanes == j
        row = a_ref[pl.ds(j, 1), :]
        root = jnp.sqrt(pick(row, at))
        col_j = jnp.where(lanes >= j, row / root, 0.0)
        lt_ref[pl.ds(j, 1), :] = col_j
        yj = pick(rhs, at) / root
        rhs = rhs - yj * col_j
        forward = jnp.where(at, yj, forward)
        diag = jnp.where(at, root, diag)
        column = jnp.sum(jnp.where(lanes == j, a_ref[...], 0.0), axis=1, keepdims=True) / root
        column = jnp.where(sublanes >= j, column, 0.0)
        a_ref[...] = a_ref[...] - column * col_j
        return rhs, forward, diag

    zeros = jnp.zeros((1, n), jnp.float32)
    _, forward, diag = lax.fori_loop(0, n, factor_step, (c_ref[...], zeros, zeros))

    def back_step(t, x):
        j = n - 1 - t
        at = lanes == j
        partial = jnp.sum(lt_ref[pl.ds(j, 1), :] * x, axis=1, keepdims=True)
        return jnp.where(at, (pick(forward, at) - partial) / pick(diag, at), x)

    x_ref[...] = lax.fori_loop(0, n, back_step, zeros)


def ridge_solve_kernel(system, cross_sum, interpret=False):
    n = system.shape[0]
    return pl.pallas_call(
        solve_kernel,
        in_specs=[pl.BlockSpec(memory_space=pltpu.VMEM), pl.BlockSpec(memory_space=pltpu.VMEM)],
        out_specs=pl.BlockSpec(memory_space=pltpu.VMEM),
        out_shape=jax.ShapeDtypeStruct((1, n), jnp.float32),
        scratch_shapes=[pltpu.VMEM((n, n), jnp.float32), pltpu.VMEM((n, n), jnp.float32)],
        interpret=interpret,
    )(system, cross_sum.reshape(1, n))[0]


def ridge_solve(system, cross_sum):
    factor = jnp.linalg.cholesky(system)
    middle = lax.linalg.triangular_solve(factor, cross_sum[:, None], left_side=True, lower=True)
    answer = lax.linalg.triangular_solve(
        factor, middle, left_side=True, lower=True, transpose_a=True
    )
    return answer[:, 0]


def butterfly_sum(x, axes):
    size = 1
    for name in axes:
        size *= lax.axis_size(name)
    if size & (size - 1):
        return lax.psum(x, axes)
    step = 1
    while step < size:
        x = x + lax.ppermute(x, axes, [(i, i ^ step) for i in range(size)])
        step *= 2
    return x


def reduce_system(gram_sum, cross_sum, axes):
    n = gram_sum.shape[0]
    h = n // 2
    rows = lax.broadcasted_iota(jnp.int32, (h, h), 0)
    cols = lax.broadcasted_iota(jnp.int32, (h, h), 1)
    lead, off, trail = gram_sum[:h, :h], gram_sum[:h, h:], gram_sum[h:, h:]
    folded = jnp.where(rows <= cols, lead, trail)
    extra = jnp.stack([cross_sum, jnp.concatenate([jnp.diagonal(trail), jnp.zeros((n - h,), jnp.float32)])])
    packed = jnp.concatenate([jnp.concatenate([folded, off], 1), extra], 0)
    packed = butterfly_sum(packed, axes)
    folded, off = packed[:h, :h], packed[:h, h:]
    upper = jnp.where(rows <= cols, folded, 0.0)
    lead = upper + jnp.where(rows < cols, folded, 0.0).T
    strict = jnp.where(rows > cols, folded, 0.0)
    trail = strict + strict.T + jnp.diag(packed[h + 1, :h])
    gram_sum = jnp.concatenate(
        [jnp.concatenate([lead, off], 1), jnp.concatenate([off.T, trail], 1)], 0
    )
    return gram_sum, packed[h]


def local(stream, target, depthwise_taps):
    length = stream.shape[1]
    top_dilation = min(1024, length // 16)
    history_len = 15 * top_dilation + 1
    tail_end = stream[:, length - history_len :]
    previous = shifted(tail_end, ("wide", "narrow"), 1)
    window = jnp.concatenate([previous, stream], 1)[:, : history_len - 1 + length]
    features, gram_sum, cross_sum = features_and_sums(window, depthwise_taps, target, top_dilation, length)
    cross_sum = cross_sum[0]
    gram_sum, cross_sum = reduce_system(gram_sum, cross_sum, ("wide", "narrow"))
    total_rows = length * lax.axis_size("wide") * lax.axis_size("narrow")
    system = gram_sum + ridge_share * total_rows * jnp.eye(gram_sum.shape[0], dtype=jnp.float32)
    coefficients = ridge_solve_kernel(system, cross_sum)
    rounded = coefficients.astype(jnp.bfloat16)
    fitted = jnp.dot(rounded, features, preferred_element_type=jnp.float32)
    return (coefficients, target.astype(jnp.float32) - fitted)


def solution(mesh):
    in_specs = (P(None, ("wide", "narrow")), P(("wide", "narrow")), P())
    out_specs = (P(), P(("wide", "narrow")))
    return jax.shard_map(local, mesh=mesh, in_specs=in_specs, out_specs=out_specs, check_vma=False)
```

```python
import functools

import jax
import jax.numpy as jnp
from jax import lax
from jax.sharding import PartitionSpec as P
from jax.experimental import pallas as pl
from jax.experimental.pallas import tpu as pltpu

ridge_share = 0.05


def shifted(array, axis, by):
    size = lax.axis_size(axis)
    pairs = [(i, i + by) for i in range(size) if 0 <= i + by < size]
    return lax.ppermute(array, axis, pairs)


def dilation_list(top_dilation):
    return (1, top_dilation // 16, top_dilation // 4, top_dilation)


def filter_bank(window, depthwise_taps, top_dilation, history_len, length):
    row_list = []
    for j, d in enumerate(dilation_list(top_dilation)):
        total = jnp.zeros((window.shape[0], length), jnp.float32)
        for k in range(depthwise_taps.shape[1]):
            start_offset = history_len - 1 - k * d
            total = (
                total
                + depthwise_taps[j, k][:, None] * window[:, start_offset : start_offset + length]
            )
        row_list.append(total.astype(jnp.bfloat16))
    return jnp.concatenate(row_list, 0)


TIME_BLOCK = 2048
ROW_GROUP = 16
NARROW_CHUNK = 1024
WIDE_CHUNK = 1024


def feature_kernel(dilations, span, base, first_block, taps_per_filter, w_ref, taps_ref, tgt_ref, f_ref, g_ref, c_ref):
    block = pl.program_id(0)
    block_len = f_ref.shape[1]
    channels = w_ref.shape[0]
    group = ROW_GROUP

    @pl.when(block == 0)
    def _():
        g_ref[...] = jnp.zeros_like(g_ref)
        c_ref[...] = jnp.zeros_like(c_ref)

    for j, d in enumerate(dilations):
        chunk = min(block_len, NARROW_CHUNK if d % 64 else WIDE_CHUNK)
        for g in range(channels // group):
            rows = pl.ds(g * group, group)

            def chunk_body(i, carry, j=j, d=d, rows=rows, g=g, chunk=chunk):
                start = pl.multiple_of((first_block + block) * block_len + i * chunk, 128)
                slabs = {}
                acc = None
                for k in range(taps_per_filter):
                    offset = span - k * d - base
                    r = offset % 128
                    a = offset - r
                    if r == 0:
                        x = w_ref[rows, pl.ds(pl.multiple_of(start + a, 128), chunk)].astype(jnp.float32)
                    else:
                        if a not in slabs:
                            slabs[a] = w_ref[rows, pl.ds(pl.multiple_of(start + a, 128), chunk + 128)].astype(jnp.float32)
                        x = slabs[a][:, r:r + chunk]
                    w = jnp.tile(taps_ref[j * taps_per_filter + k, rows, :], (1, chunk // 128))
                    acc = w * x if acc is None else acc + w * x
                out_rows = pl.ds(j * channels + g * group, group)
                f_ref[out_rows, pl.ds(pl.multiple_of(i * chunk, 128), chunk)] = acc.astype(f_ref.dtype)
                return carry

            lax.fori_loop(0, block_len // chunk, chunk_body, 0)

    feats = f_ref[...]
    g_ref[...] += lax.dot_general(feats, feats, (((1,), (1,)), ((), ())), preferred_element_type=jnp.float32)
    c_ref[...] += lax.dot_general(tgt_ref[...], feats, (((1,), (1,)), ((), ())), preferred_element_type=jnp.float32)


def features_and_sums(window, base, first_block, n_blocks, depthwise_taps, target, top_dilation, length, interpret=False):
    channels = window.shape[0]
    dilations = dilation_list(top_dilation)
    n_filters, taps_per_filter = len(dilations), depthwise_taps.shape[1]
    span = (taps_per_filter - 1) * top_dilation
    rows = n_filters * channels
    block_len = min(TIME_BLOCK, length)
    taps = jnp.broadcast_to(
        depthwise_taps.reshape(n_filters * taps_per_filter, channels, 1),
        (n_filters * taps_per_filter, channels, 128),
    )
    kernel = functools.partial(feature_kernel, dilations, span, base, first_block, taps_per_filter)
    return pl.pallas_call(
        kernel,
        grid=(n_blocks,),
        in_specs=[
            pl.BlockSpec(memory_space=pltpu.VMEM),
            pl.BlockSpec(memory_space=pltpu.VMEM),
            pl.BlockSpec((1, block_len), lambda b: (0, b + first_block)),
        ],
        out_specs=[
            pl.BlockSpec((rows, block_len), lambda b: (0, b)),
            pl.BlockSpec((rows, rows), lambda b: (0, 0)),
            pl.BlockSpec((1, rows), lambda b: (0, 0)),
        ],
        out_shape=[
            jax.ShapeDtypeStruct((rows, n_blocks * block_len), jnp.bfloat16),
            jax.ShapeDtypeStruct((rows, rows), jnp.float32),
            jax.ShapeDtypeStruct((1, rows), jnp.float32),
        ],
        compiler_params=pltpu.CompilerParams(
            dimension_semantics=("arbitrary",), vmem_limit_bytes=48 * 1024 * 1024
        ),
        interpret=interpret,
    )(window, taps, target.reshape(1, length))


def solve_kernel(system_ref, c_ref, x_ref, a_ref, lt_ref):
    n = a_ref.shape[0]
    a_ref[...] = system_ref[...]
    lanes = lax.broadcasted_iota(jnp.int32, (1, n), 1)
    sublanes = lax.broadcasted_iota(jnp.int32, (n, 1), 0)

    def pick(vec, at):
        return jnp.sum(jnp.where(at, vec, 0.0), axis=1, keepdims=True)

    def factor_step(j, carry):
        rhs, forward, diag = carry
        at = lanes == j
        row = a_ref[pl.ds(j, 1), :]
        root = jnp.sqrt(pick(row, at))
        col_j = jnp.where(lanes >= j, row / root, 0.0)
        lt_ref[pl.ds(j, 1), :] = col_j
        yj = pick(rhs, at) / root
        rhs = rhs - yj * col_j
        forward = jnp.where(at, yj, forward)
        diag = jnp.where(at, root, diag)
        column = jnp.sum(jnp.where(lanes == j, a_ref[...], 0.0), axis=1, keepdims=True) / root
        column = jnp.where(sublanes >= j, column, 0.0)
        a_ref[...] = a_ref[...] - column * col_j
        return rhs, forward, diag

    zeros = jnp.zeros((1, n), jnp.float32)
    _, forward, diag = lax.fori_loop(0, n, factor_step, (c_ref[...], zeros, zeros))

    def back_step(t, x):
        j = n - 1 - t
        at = lanes == j
        partial = jnp.sum(lt_ref[pl.ds(j, 1), :] * x, axis=1, keepdims=True)
        return jnp.where(at, (pick(forward, at) - partial) / pick(diag, at), x)

    x_ref[...] = lax.fori_loop(0, n, back_step, zeros)


def ridge_solve_kernel(system, cross_sum, interpret=False):
    n = system.shape[0]
    return pl.pallas_call(
        solve_kernel,
        in_specs=[pl.BlockSpec(memory_space=pltpu.VMEM), pl.BlockSpec(memory_space=pltpu.VMEM)],
        out_specs=pl.BlockSpec(memory_space=pltpu.VMEM),
        out_shape=jax.ShapeDtypeStruct((1, n), jnp.float32),
        scratch_shapes=[pltpu.VMEM((n, n), jnp.float32), pltpu.VMEM((n, n), jnp.float32)],
        interpret=interpret,
    )(system, cross_sum.reshape(1, n))[0]


def ridge_solve(system, cross_sum):
    factor = jnp.linalg.cholesky(system)
    middle = lax.linalg.triangular_solve(factor, cross_sum[:, None], left_side=True, lower=True)
    answer = lax.linalg.triangular_solve(
        factor, middle, left_side=True, lower=True, transpose_a=True
    )
    return answer[:, 0]


def butterfly_sum(x, axes):
    size = 1
    for name in axes:
        size *= lax.axis_size(name)
    if size & (size - 1):
        return lax.psum(x, axes)
    step = 1
    while step < size:
        x = x + lax.ppermute(x, axes, [(i, i ^ step) for i in range(size)])
        step *= 2
    return x


def reduce_system(gram_sum, cross_sum, axes):
    n = gram_sum.shape[0]
    h = n // 2
    rows = lax.broadcasted_iota(jnp.int32, (h, h), 0)
    cols = lax.broadcasted_iota(jnp.int32, (h, h), 1)
    lead, off, trail = gram_sum[:h, :h], gram_sum[:h, h:], gram_sum[h:, h:]
    folded = jnp.where(rows <= cols, lead, trail)
    extra = jnp.stack([cross_sum, jnp.concatenate([jnp.diagonal(trail), jnp.zeros((n - h,), jnp.float32)])])
    packed = jnp.concatenate([jnp.concatenate([folded, off], 1), extra], 0)
    packed = butterfly_sum(packed, axes)
    folded, off = packed[:h, :h], packed[:h, h:]
    upper = jnp.where(rows <= cols, folded, 0.0)
    lead = upper + jnp.where(rows < cols, folded, 0.0).T
    strict = jnp.where(rows > cols, folded, 0.0)
    trail = strict + strict.T + jnp.diag(packed[h + 1, :h])
    gram_sum = jnp.concatenate(
        [jnp.concatenate([lead, off], 1), jnp.concatenate([off.T, trail], 1)], 0
    )
    return gram_sum, packed[h]


def local(stream, target, depthwise_taps):
    length = stream.shape[1]
    top_dilation = min(1024, length // 16)
    history_len = 15 * top_dilation + 1
    tail_end = stream[:, length - history_len :]
    previous = shifted(tail_end, ("wide", "narrow"), 1)
    span = history_len - 1
    block_len = min(TIME_BLOCK, length)
    n_blocks = length // block_len
    split = min(n_blocks, -(-span // block_len))
    window = jnp.concatenate([previous, stream], 1)[:, : split * block_len + span]
    features, gram_sum, cross_sum = features_and_sums(
        window, 0, 0, split, depthwise_taps, target, top_dilation, length
    )
    if split < n_blocks:
        delayed = jnp.concatenate([jnp.zeros_like(stream[:, :1]), stream[:, : length - 1]], 1)
        late_features, late_gram, late_cross = features_and_sums(
            delayed, span, split, n_blocks - split, depthwise_taps, target, top_dilation, length
        )
        features = (features, late_features)
        gram_sum, cross_sum = gram_sum + late_gram, cross_sum + late_cross
    else:
        features = (features,)
    cross_sum = cross_sum[0]
    gram_sum, cross_sum = reduce_system(gram_sum, cross_sum, ("wide", "narrow"))
    total_rows = length * lax.axis_size("wide") * lax.axis_size("narrow")
    system = gram_sum + ridge_share * total_rows * jnp.eye(gram_sum.shape[0], dtype=jnp.float32)
    coefficients = ridge_solve_kernel(system, cross_sum)
    rounded = coefficients.astype(jnp.bfloat16)
    fitted = jnp.concatenate([jnp.dot(rounded, f, preferred_element_type=jnp.float32) for f in features])
    return (coefficients, target.astype(jnp.float32) - fitted)


def solution(mesh):
    in_specs = (P(None, ("wide", "narrow")), P(("wide", "narrow")), P())
    out_specs = (P(), P(("wide", "narrow")))
    return jax.shard_map(local, mesh=mesh, in_specs=in_specs, out_specs=out_specs, check_vma=False)
```

```python
import functools

import jax
import jax.numpy as jnp
from jax import lax
from jax.sharding import PartitionSpec as P
from jax.experimental import pallas as pl
from jax.experimental.pallas import tpu as pltpu

ridge_share = 0.05


def shifted(array, axis, by):
    size = lax.axis_size(axis)
    pairs = [(i, i + by) for i in range(size) if 0 <= i + by < size]
    return lax.ppermute(array, axis, pairs)


def dilation_list(top_dilation):
    return (1, top_dilation // 16, top_dilation // 4, top_dilation)


def filter_bank(window, depthwise_taps, top_dilation, history_len, length):
    row_list = []
    for j, d in enumerate(dilation_list(top_dilation)):
        total = jnp.zeros((window.shape[0], length), jnp.float32)
        for k in range(depthwise_taps.shape[1]):
            start_offset = history_len - 1 - k * d
            total = (
                total
                + depthwise_taps[j, k][:, None] * window[:, start_offset : start_offset + length]
            )
        row_list.append(total.astype(jnp.bfloat16))
    return jnp.concatenate(row_list, 0)


TIME_BLOCK = 2048
ROW_GROUP = 16
NARROW_CHUNK = 1024
WIDE_CHUNK = 1024


def feature_kernel(dilations, span, base, first_block, taps_per_filter, w_ref, taps_ref, tgt_ref, f_ref, g_ref, c_ref):
    block = pl.program_id(0)
    block_len = f_ref.shape[1]
    channels = w_ref.shape[0]
    group = ROW_GROUP

    @pl.when(block == 0)
    def _():
        g_ref[...] = jnp.zeros_like(g_ref)
        c_ref[...] = jnp.zeros_like(c_ref)

    for j, d in enumerate(dilations):
        chunk = min(block_len, NARROW_CHUNK if d % 64 else WIDE_CHUNK)
        for g in range(channels // group):
            rows = pl.ds(g * group, group)

            def chunk_body(i, carry, j=j, d=d, rows=rows, g=g, chunk=chunk):
                start = pl.multiple_of((first_block + block) * block_len + i * chunk, 128)
                slabs = {}
                acc = None
                for k in range(taps_per_filter):
                    offset = span - k * d - base
                    r = offset % 128
                    a = offset - r
                    if r == 0:
                        x = w_ref[rows, pl.ds(pl.multiple_of(start + a, 128), chunk)].astype(jnp.float32)
                    else:
                        if a not in slabs:
                            slabs[a] = w_ref[rows, pl.ds(pl.multiple_of(start + a, 128), chunk + 128)].astype(jnp.float32)
                        x = slabs[a][:, r:r + chunk]
                    w = jnp.tile(taps_ref[j * taps_per_filter + k, rows, :], (1, chunk // 128))
                    acc = w * x if acc is None else acc + w * x
                out_rows = pl.ds(j * channels + g * group, group)
                f_ref[out_rows, pl.ds(pl.multiple_of(i * chunk, 128), chunk)] = acc.astype(f_ref.dtype)
                return carry

            lax.fori_loop(0, block_len // chunk, chunk_body, 0)

    feats = f_ref[...]
    g_ref[...] += lax.dot_general(feats, feats, (((1,), (1,)), ((), ())), preferred_element_type=jnp.float32)
    c_ref[...] += lax.dot_general(tgt_ref[...], feats, (((1,), (1,)), ((), ())), preferred_element_type=jnp.float32)


def features_and_sums(window, base, first_block, n_blocks, depthwise_taps, target, top_dilation, length, interpret=False):
    channels = window.shape[0]
    dilations = dilation_list(top_dilation)
    n_filters, taps_per_filter = len(dilations), depthwise_taps.shape[1]
    span = (taps_per_filter - 1) * top_dilation
    rows = n_filters * channels
    block_len = min(TIME_BLOCK, length)
    taps = jnp.broadcast_to(
        depthwise_taps.reshape(n_filters * taps_per_filter, channels, 1),
        (n_filters * taps_per_filter, channels, 128),
    )
    kernel = functools.partial(feature_kernel, dilations, span, base, first_block, taps_per_filter)
    return pl.pallas_call(
        kernel,
        grid=(n_blocks,),
        in_specs=[
            pl.BlockSpec(memory_space=pltpu.VMEM),
            pl.BlockSpec(memory_space=pltpu.VMEM),
            pl.BlockSpec((1, block_len), lambda b: (0, b + first_block)),
        ],
        out_specs=[
            pl.BlockSpec((rows, block_len), lambda b: (0, b)),
            pl.BlockSpec((rows, rows), lambda b: (0, 0)),
            pl.BlockSpec((1, rows), lambda b: (0, 0)),
        ],
        out_shape=[
            jax.ShapeDtypeStruct((rows, n_blocks * block_len), jnp.bfloat16),
            jax.ShapeDtypeStruct((rows, rows), jnp.float32),
            jax.ShapeDtypeStruct((1, rows), jnp.float32),
        ],
        compiler_params=pltpu.CompilerParams(
            dimension_semantics=("arbitrary",), vmem_limit_bytes=48 * 1024 * 1024
        ),
        interpret=interpret,
    )(window, taps, target.reshape(1, length))


def solve_kernel(system_ref, c_ref, x_ref, a_ref, lt_ref):
    n = a_ref.shape[0]
    a_ref[...] = system_ref[...]
    lanes = lax.broadcasted_iota(jnp.int32, (1, n), 1)
    sublanes = lax.broadcasted_iota(jnp.int32, (n, 1), 0)

    def pick(vec, at):
        return jnp.sum(jnp.where(at, vec, 0.0), axis=1, keepdims=True)

    def factor_step(j, carry):
        rhs, forward, diag = carry
        at = lanes == j
        row = a_ref[pl.ds(j, 1), :]
        root = jnp.sqrt(pick(row, at))
        col_j = jnp.where(lanes >= j, row / root, 0.0)
        lt_ref[pl.ds(j, 1), :] = col_j
        yj = pick(rhs, at) / root
        rhs = rhs - yj * col_j
        forward = jnp.where(at, yj, forward)
        diag = jnp.where(at, root, diag)
        column = jnp.sum(jnp.where(lanes == j, a_ref[...], 0.0), axis=1, keepdims=True) / root
        column = jnp.where(sublanes >= j, column, 0.0)
        a_ref[...] = a_ref[...] - column * col_j
        return rhs, forward, diag

    zeros = jnp.zeros((1, n), jnp.float32)
    _, forward, diag = lax.fori_loop(0, n, factor_step, (c_ref[...], zeros, zeros))

    def back_step(t, x):
        j = n - 1 - t
        at = lanes == j
        partial = jnp.sum(lt_ref[pl.ds(j, 1), :] * x, axis=1, keepdims=True)
        return jnp.where(at, (pick(forward, at) - partial) / pick(diag, at), x)

    x_ref[...] = lax.fori_loop(0, n, back_step, zeros)


def ridge_solve_kernel(system, cross_sum, interpret=False):
    n = system.shape[0]
    return pl.pallas_call(
        solve_kernel,
        in_specs=[pl.BlockSpec(memory_space=pltpu.VMEM), pl.BlockSpec(memory_space=pltpu.VMEM)],
        out_specs=pl.BlockSpec(memory_space=pltpu.VMEM),
        out_shape=jax.ShapeDtypeStruct((1, n), jnp.float32),
        scratch_shapes=[pltpu.VMEM((n, n), jnp.float32), pltpu.VMEM((n, n), jnp.float32)],
        interpret=interpret,
    )(system, cross_sum.reshape(1, n))[0]


def jordan_kernel(system_ref, c_ref, x_ref, a_ref):
    n = a_ref.shape[0]
    a_ref[...] = system_ref[...]
    x_ref[...] = c_ref[...]
    lanes = lax.broadcasted_iota(jnp.int32, (1, n), 1)
    sublanes = lax.broadcasted_iota(jnp.int32, (n, 1), 0)

    def step(j, carry):
        at = lanes == j
        here = sublanes == j
        row = a_ref[pl.ds(j, 1), :]
        pivot = jnp.sum(jnp.where(at, row, 0.0), axis=1, keepdims=True)
        column = jnp.sum(jnp.where(at, a_ref[...], 0.0), axis=1, keepdims=True)
        scaled_row = row / pivot
        scaled_rhs = x_ref[pl.ds(j, 1), :] / pivot
        a_ref[...] = jnp.where(here, scaled_row, a_ref[...] - column * scaled_row)
        x_ref[...] = jnp.where(here, scaled_rhs, x_ref[...] - column * scaled_rhs)
        return carry

    lax.fori_loop(0, n, step, 0)


def ridge_solve_jordan(system, cross_sum, interpret=False):
    n = system.shape[0]
    rhs = jnp.broadcast_to(cross_sum[:, None], (n, 128))
    return pl.pallas_call(
        jordan_kernel,
        in_specs=[pl.BlockSpec(memory_space=pltpu.VMEM), pl.BlockSpec(memory_space=pltpu.VMEM)],
        out_specs=pl.BlockSpec(memory_space=pltpu.VMEM),
        out_shape=jax.ShapeDtypeStruct((n, 128), jnp.float32),
        scratch_shapes=[pltpu.VMEM((n, n), jnp.float32)],
        interpret=interpret,
    )(system, rhs)[:, 0]


def ridge_solve(system, cross_sum):
    factor = jnp.linalg.cholesky(system)
    middle = lax.linalg.triangular_solve(factor, cross_sum[:, None], left_side=True, lower=True)
    answer = lax.linalg.triangular_solve(
        factor, middle, left_side=True, lower=True, transpose_a=True
    )
    return answer[:, 0]


def butterfly_sum(x, axes):
    size = 1
    for name in axes:
        size *= lax.axis_size(name)
    if size & (size - 1):
        return lax.psum(x, axes)
    step = 1
    while step < size:
        x = x + lax.ppermute(x, axes, [(i, i ^ step) for i in range(size)])
        step *= 2
    return x


def reduce_system(gram_sum, cross_sum, axes):
    n = gram_sum.shape[0]
    h = n // 2
    rows = lax.broadcasted_iota(jnp.int32, (h, h), 0)
    cols = lax.broadcasted_iota(jnp.int32, (h, h), 1)
    lead, off, trail = gram_sum[:h, :h], gram_sum[:h, h:], gram_sum[h:, h:]
    folded = jnp.where(rows <= cols, lead, trail)
    extra = jnp.stack([cross_sum, jnp.concatenate([jnp.diagonal(trail), jnp.zeros((n - h,), jnp.float32)])])
    packed = jnp.concatenate([jnp.concatenate([folded, off], 1), extra], 0)
    packed = butterfly_sum(packed, axes)
    folded, off = packed[:h, :h], packed[:h, h:]
    upper = jnp.where(rows <= cols, folded, 0.0)
    lead = upper + jnp.where(rows < cols, folded, 0.0).T
    strict = jnp.where(rows > cols, folded, 0.0)
    trail = strict + strict.T + jnp.diag(packed[h + 1, :h])
    gram_sum = jnp.concatenate(
        [jnp.concatenate([lead, off], 1), jnp.concatenate([off.T, trail], 1)], 0
    )
    return gram_sum, packed[h]


def local(stream, target, depthwise_taps):
    length = stream.shape[1]
    top_dilation = min(1024, length // 16)
    history_len = 15 * top_dilation + 1
    tail_end = stream[:, length - history_len :]
    previous = shifted(tail_end, ("wide", "narrow"), 1)
    span = history_len - 1
    block_len = min(TIME_BLOCK, length)
    n_blocks = length // block_len
    split = min(n_blocks, -(-span // block_len))
    window = jnp.concatenate([previous, stream], 1)[:, : split * block_len + span]
    features, gram_sum, cross_sum = features_and_sums(
        window, 0, 0, split, depthwise_taps, target, top_dilation, length
    )
    if split < n_blocks:
        delayed = jnp.concatenate([jnp.zeros_like(stream[:, :1]), stream[:, : length - 1]], 1)
        late_features, late_gram, late_cross = features_and_sums(
            delayed, span, split, n_blocks - split, depthwise_taps, target, top_dilation, length
        )
        features = (features, late_features)
        gram_sum, cross_sum = gram_sum + late_gram, cross_sum + late_cross
    else:
        features = (features,)
    cross_sum = cross_sum[0]
    gram_sum, cross_sum = reduce_system(gram_sum, cross_sum, ("wide", "narrow"))
    total_rows = length * lax.axis_size("wide") * lax.axis_size("narrow")
    system = gram_sum + ridge_share * total_rows * jnp.eye(gram_sum.shape[0], dtype=jnp.float32)
    coefficients = ridge_solve_jordan(system, cross_sum)
    rounded = coefficients.astype(jnp.bfloat16)
    fitted = jnp.concatenate([jnp.dot(rounded, f, preferred_element_type=jnp.float32) for f in features])
    return (coefficients, target.astype(jnp.float32) - fitted)


def solution(mesh):
    in_specs = (P(None, ("wide", "narrow")), P(("wide", "narrow")), P())
    out_specs = (P(), P(("wide", "narrow")))
    return jax.shard_map(local, mesh=mesh, in_specs=in_specs, out_specs=out_specs, check_vma=False)
```

```python
import functools

import jax
import jax.numpy as jnp
from jax import lax
from jax.sharding import PartitionSpec as P
from jax.experimental import pallas as pl
from jax.experimental.pallas import tpu as pltpu

ridge_share = 0.05


def shifted(array, axis, by):
    size = lax.axis_size(axis)
    pairs = [(i, i + by) for i in range(size) if 0 <= i + by < size]
    return lax.ppermute(array, axis, pairs)


def dilation_list(top_dilation):
    return (1, top_dilation // 16, top_dilation // 4, top_dilation)


def filter_bank(window, depthwise_taps, top_dilation, history_len, length):
    row_list = []
    for j, d in enumerate(dilation_list(top_dilation)):
        total = jnp.zeros((window.shape[0], length), jnp.float32)
        for k in range(depthwise_taps.shape[1]):
            start_offset = history_len - 1 - k * d
            total = (
                total
                + depthwise_taps[j, k][:, None] * window[:, start_offset : start_offset + length]
            )
        row_list.append(total.astype(jnp.bfloat16))
    return jnp.concatenate(row_list, 0)


TIME_BLOCK = 2048
ROW_GROUP = 16
NARROW_CHUNK = 1024
WIDE_CHUNK = 1024


def feature_kernel(dilations, span, base, first_block, length, taps_per_filter, w_ref, taps_ref, tgt_ref, f_ref, g_ref, c_ref):
    block = pl.program_id(0)
    block_len = f_ref.shape[1]
    channels = w_ref.shape[0]
    group = ROW_GROUP

    @pl.when(block == 0)
    def _():
        g_ref[...] = jnp.zeros_like(g_ref)
        c_ref[...] = jnp.zeros_like(c_ref)

    for j, d in enumerate(dilations):
        chunk = min(block_len, NARROW_CHUNK if d % 64 else WIDE_CHUNK)
        for g in range(channels // group):
            rows = pl.ds(g * group, group)

            def chunk_body(i, carry, j=j, d=d, rows=rows, g=g, chunk=chunk):
                start = pl.multiple_of((first_block + block) * block_len + i * chunk, 128)
                slabs = {}
                acc = None
                for k in range(taps_per_filter):
                    offset = span - k * d - base
                    r = offset % 128
                    a = offset - r
                    if r == 0:
                        x = w_ref[rows, pl.ds(pl.multiple_of(start + a, 128), chunk)].astype(jnp.float32)
                    else:
                        if a not in slabs:
                            slabs[a] = w_ref[rows, pl.ds(pl.multiple_of(start + a, 128), chunk + 128)].astype(jnp.float32)
                        x = slabs[a][:, r:r + chunk]
                    w = jnp.tile(taps_ref[j * taps_per_filter + k, rows, :], (1, chunk // 128))
                    acc = w * x if acc is None else acc + w * x
                out_rows = pl.ds(j * channels + g * group, group)
                f_ref[out_rows, pl.ds(pl.multiple_of(i * chunk, 128), chunk)] = acc.astype(f_ref.dtype)
                return carry

            lax.fori_loop(0, block_len // chunk, chunk_body, 0)

    cols = (first_block + block) * block_len + lax.broadcasted_iota(jnp.int32, (1, block_len), 1)
    feats = jnp.where(cols < length - 1, f_ref[...], jnp.zeros_like(f_ref[...]))
    g_ref[...] += lax.dot_general(feats, feats, (((1,), (1,)), ((), ())), preferred_element_type=jnp.float32)
    c_ref[...] += lax.dot_general(tgt_ref[...], feats, (((1,), (1,)), ((), ())), preferred_element_type=jnp.float32)


def features_and_sums(window, base, first_block, n_blocks, depthwise_taps, target, top_dilation, length, interpret=False):
    channels = window.shape[0]
    dilations = dilation_list(top_dilation)
    n_filters, taps_per_filter = len(dilations), depthwise_taps.shape[1]
    span = (taps_per_filter - 1) * top_dilation
    rows = n_filters * channels
    block_len = min(TIME_BLOCK, length)
    taps = jnp.broadcast_to(
        depthwise_taps.reshape(n_filters * taps_per_filter, channels, 1),
        (n_filters * taps_per_filter, channels, 128),
    )
    kernel = functools.partial(feature_kernel, dilations, span, base, first_block, length, taps_per_filter)
    return pl.pallas_call(
        kernel,
        grid=(n_blocks,),
        in_specs=[
            pl.BlockSpec(memory_space=pltpu.VMEM),
            pl.BlockSpec(memory_space=pltpu.VMEM),
            pl.BlockSpec((1, block_len), lambda b: (0, b + first_block)),
        ],
        out_specs=[
            pl.BlockSpec((rows, block_len), lambda b: (0, b)),
            pl.BlockSpec((rows, rows), lambda b: (0, 0)),
            pl.BlockSpec((1, rows), lambda b: (0, 0)),
        ],
        out_shape=[
            jax.ShapeDtypeStruct((rows, n_blocks * block_len), jnp.bfloat16),
            jax.ShapeDtypeStruct((rows, rows), jnp.float32),
            jax.ShapeDtypeStruct((1, rows), jnp.float32),
        ],
        compiler_params=pltpu.CompilerParams(
            dimension_semantics=("arbitrary",), vmem_limit_bytes=48 * 1024 * 1024
        ),
        interpret=interpret,
    )(window, taps, target.reshape(1, length))


def solve_kernel(system_ref, c_ref, x_ref, a_ref, lt_ref):
    n = a_ref.shape[0]
    a_ref[...] = system_ref[...]
    lanes = lax.broadcasted_iota(jnp.int32, (1, n), 1)
    sublanes = lax.broadcasted_iota(jnp.int32, (n, 1), 0)

    def pick(vec, at):
        return jnp.sum(jnp.where(at, vec, 0.0), axis=1, keepdims=True)

    def factor_step(j, carry):
        rhs, forward, diag = carry
        at = lanes == j
        row = a_ref[pl.ds(j, 1), :]
        root = jnp.sqrt(pick(row, at))
        col_j = jnp.where(lanes >= j, row / root, 0.0)
        lt_ref[pl.ds(j, 1), :] = col_j
        yj = pick(rhs, at) / root
        rhs = rhs - yj * col_j
        forward = jnp.where(at, yj, forward)
        diag = jnp.where(at, root, diag)
        column = jnp.sum(jnp.where(lanes == j, a_ref[...], 0.0), axis=1, keepdims=True) / root
        column = jnp.where(sublanes >= j, column, 0.0)
        a_ref[...] = a_ref[...] - column * col_j
        return rhs, forward, diag

    zeros = jnp.zeros((1, n), jnp.float32)
    _, forward, diag = lax.fori_loop(0, n, factor_step, (c_ref[...], zeros, zeros))

    def back_step(t, x):
        j = n - 1 - t
        at = lanes == j
        partial = jnp.sum(lt_ref[pl.ds(j, 1), :] * x, axis=1, keepdims=True)
        return jnp.where(at, (pick(forward, at) - partial) / pick(diag, at), x)

    x_ref[...] = lax.fori_loop(0, n, back_step, zeros)


def ridge_solve_kernel(system, cross_sum, interpret=False):
    n = system.shape[0]
    return pl.pallas_call(
        solve_kernel,
        in_specs=[pl.BlockSpec(memory_space=pltpu.VMEM), pl.BlockSpec(memory_space=pltpu.VMEM)],
        out_specs=pl.BlockSpec(memory_space=pltpu.VMEM),
        out_shape=jax.ShapeDtypeStruct((1, n), jnp.float32),
        scratch_shapes=[pltpu.VMEM((n, n), jnp.float32), pltpu.VMEM((n, n), jnp.float32)],
        interpret=interpret,
    )(system, cross_sum.reshape(1, n))[0]


def jordan_kernel(system_ref, c_ref, x_ref, a_ref):
    n = a_ref.shape[0]
    a_ref[...] = system_ref[...]
    x_ref[...] = c_ref[...]
    sublanes = lax.broadcasted_iota(jnp.int32, (n, 1), 0)

    for lo in range(0, n, 128):
        lanes = lo + lax.broadcasted_iota(jnp.int32, (1, n - lo), 1)

        def step(j, carry, lo=lo, lanes=lanes):
            at = lanes == j
            here = sublanes == j
            row = a_ref[pl.ds(j, 1), :][:, lo:]
            pivot = jnp.sum(jnp.where(at, row, 0.0), axis=1, keepdims=True)
            column = jnp.sum(jnp.where(at, a_ref[:, lo:], 0.0), axis=1, keepdims=True)
            scaled_row = row / pivot
            scaled_rhs = x_ref[pl.ds(j, 1), :] / pivot
            a_ref[:, lo:] = jnp.where(here, scaled_row, a_ref[:, lo:] - column * scaled_row)
            x_ref[...] = jnp.where(here, scaled_rhs, x_ref[...] - column * scaled_rhs)
            return carry

        lax.fori_loop(lo, min(n, lo + 128), step, 0)


def ridge_solve_jordan(system, cross_sum, interpret=False):
    n = system.shape[0]
    rhs = jnp.broadcast_to(cross_sum[:, None], (n, 128))
    return pl.pallas_call(
        jordan_kernel,
        in_specs=[pl.BlockSpec(memory_space=pltpu.VMEM), pl.BlockSpec(memory_space=pltpu.VMEM)],
        out_specs=pl.BlockSpec(memory_space=pltpu.VMEM),
        out_shape=jax.ShapeDtypeStruct((n, 128), jnp.float32),
        scratch_shapes=[pltpu.VMEM((n, n), jnp.float32)],
        interpret=interpret,
    )(system, rhs)[:, 0]


def ridge_solve(system, cross_sum):
    factor = jnp.linalg.cholesky(system)
    middle = lax.linalg.triangular_solve(factor, cross_sum[:, None], left_side=True, lower=True)
    answer = lax.linalg.triangular_solve(
        factor, middle, left_side=True, lower=True, transpose_a=True
    )
    return answer[:, 0]


def butterfly_sum(x, axes):
    size = 1
    for name in axes:
        size *= lax.axis_size(name)
    if size & (size - 1):
        return lax.psum(x, axes)
    step = 1
    while step < size:
        x = x + lax.ppermute(x, axes, [(i, i ^ step) for i in range(size)])
        step *= 2
    return x


def reduce_system(gram_sum, cross_sum, axes):
    n = gram_sum.shape[0]
    h = n // 2
    rows = lax.broadcasted_iota(jnp.int32, (h, h), 0)
    cols = lax.broadcasted_iota(jnp.int32, (h, h), 1)
    lead, off, trail = gram_sum[:h, :h], gram_sum[:h, h:], gram_sum[h:, h:]
    folded = jnp.where(rows <= cols, lead, trail)
    extra = jnp.stack([cross_sum, jnp.concatenate([jnp.diagonal(trail), jnp.zeros((n - h,), jnp.float32)])])
    packed = jnp.concatenate([jnp.concatenate([folded, off], 1), extra], 0)
    packed = butterfly_sum(packed, axes)
    folded, off = packed[:h, :h], packed[:h, h:]
    upper = jnp.where(rows <= cols, folded, 0.0)
    lead = upper + jnp.where(rows < cols, folded, 0.0).T
    strict = jnp.where(rows > cols, folded, 0.0)
    trail = strict + strict.T + jnp.diag(packed[h + 1, :h])
    gram_sum = jnp.concatenate(
        [jnp.concatenate([lead, off], 1), jnp.concatenate([off.T, trail], 1)], 0
    )
    return gram_sum, packed[h]


def first_features(history, depthwise_taps, top_dilation):
    last = history.shape[1] - 1
    picks = jnp.asarray(
        [[last - k * d for k in range(depthwise_taps.shape[1])] for d in dilation_list(top_dilation)],
        jnp.int32,
    )
    samples = jnp.transpose(history[:, picks], (1, 2, 0)).astype(jnp.float32)
    total = jnp.zeros(samples.shape[::2], jnp.float32)
    for k in range(depthwise_taps.shape[1]):
        total = total + depthwise_taps[:, k] * samples[:, k]
    return total.astype(jnp.bfloat16).reshape(-1)


def local(stream, target, depthwise_taps):
    length = stream.shape[1]
    top_dilation = min(1024, length // 16)
    history_len = 15 * top_dilation + 1
    span = history_len - 1
    sent = min(length, -(-history_len // 128) * 128)
    previous = shifted(stream[:, length - sent :], ("wide", "narrow"), 1)
    block_len = min(TIME_BLOCK, length)
    n_blocks = length // block_len
    split = min(n_blocks, -(-span // block_len))
    ahead = jnp.concatenate([target[1:], jnp.zeros_like(target[:1])])
    window = jnp.concatenate([previous[:, sent - span :], stream[:, : split * block_len]], 1)
    early, gram_sum, cross_sum = features_and_sums(
        window, 0, 0, split, depthwise_taps, ahead, top_dilation, length
    )
    parts = [early]
    if split < n_blocks:
        late, late_gram, late_cross = features_and_sums(
            stream, span, split, n_blocks - split, depthwise_taps, ahead, top_dilation, length
        )
        parts.append(late)
        gram_sum, cross_sum = gram_sum + late_gram, cross_sum + late_cross
    first = first_features(previous, depthwise_taps, top_dilation).astype(jnp.float32)
    gram_sum = gram_sum + first[:, None] * first[None, :]
    cross_sum = cross_sum[0] + first * target[0].astype(jnp.float32)
    gram_sum, cross_sum = reduce_system(gram_sum, cross_sum, ("wide", "narrow"))
    total_rows = length * lax.axis_size("wide") * lax.axis_size("narrow")
    system = gram_sum + ridge_share * total_rows * jnp.eye(gram_sum.shape[0], dtype=jnp.float32)
    coefficients = ridge_solve_jordan(system, cross_sum)
    rounded = coefficients.astype(jnp.bfloat16)
    fitted = [jnp.dot(rounded, first.astype(jnp.bfloat16), preferred_element_type=jnp.float32)[None]]
    fitted += [jnp.dot(rounded, f, preferred_element_type=jnp.float32) for f in parts]
    fitted = jnp.concatenate(fitted)[:length]
    return (coefficients, target.astype(jnp.float32) - fitted)


def solution(mesh):
    in_specs = (P(None, ("wide", "narrow")), P(("wide", "narrow")), P())
    out_specs = (P(), P(("wide", "narrow")))
    return jax.shard_map(local, mesh=mesh, in_specs=in_specs, out_specs=out_specs, check_vma=False)
```

```python
import functools

import jax
import jax.numpy as jnp
from jax import lax
from jax.sharding import PartitionSpec as P
from jax.experimental import pallas as pl
from jax.experimental.pallas import tpu as pltpu

ridge_share = 0.05


def shifted(array, axis, by):
    size = lax.axis_size(axis)
    pairs = [(i, i + by) for i in range(size) if 0 <= i + by < size]
    return lax.ppermute(array, axis, pairs)


def dilation_list(top_dilation):
    return (1, top_dilation // 16, top_dilation // 4, top_dilation)


def filter_bank(window, depthwise_taps, top_dilation, history_len, length):
    row_list = []
    for j, d in enumerate(dilation_list(top_dilation)):
        total = jnp.zeros((window.shape[0], length), jnp.float32)
        for k in range(depthwise_taps.shape[1]):
            start_offset = history_len - 1 - k * d
            total = (
                total
                + depthwise_taps[j, k][:, None] * window[:, start_offset : start_offset + length]
            )
        row_list.append(total.astype(jnp.bfloat16))
    return jnp.concatenate(row_list, 0)


TIME_BLOCK = 2048
ROW_GROUP = 16
NARROW_CHUNK = 1024
WIDE_CHUNK = 1024


def feature_kernel(dilations, span, base, first_block, length, taps_per_filter, w_ref, taps_ref, tgt_ref, f_ref, g_ref, c_ref):
    block = pl.program_id(0)
    block_len = f_ref.shape[1]
    channels = w_ref.shape[0]
    group = ROW_GROUP

    @pl.when(block == 0)
    def _():
        g_ref[...] = jnp.zeros_like(g_ref)
        c_ref[...] = jnp.zeros_like(c_ref)

    for j, d in enumerate(dilations):
        chunk = min(block_len, NARROW_CHUNK if d % 64 else WIDE_CHUNK)
        for g in range(channels // group):
            rows = pl.ds(g * group, group)

            def chunk_body(i, carry, j=j, d=d, rows=rows, g=g, chunk=chunk):
                start = pl.multiple_of((first_block + block) * block_len + i * chunk, 128)
                slabs = {}
                acc = None
                for k in range(taps_per_filter):
                    offset = span - k * d - base
                    r = offset % 128
                    a = offset - r
                    if r == 0:
                        x = w_ref[rows, pl.ds(pl.multiple_of(start + a, 128), chunk)].astype(jnp.float32)
                    else:
                        if a not in slabs:
                            slabs[a] = w_ref[rows, pl.ds(pl.multiple_of(start + a, 128), chunk + 128)].astype(jnp.float32)
                        x = slabs[a][:, r:r + chunk]
                    w = jnp.tile(taps_ref[j * taps_per_filter + k, rows, :], (1, chunk // 128))
                    acc = w * x if acc is None else acc + w * x
                out_rows = pl.ds(j * channels + g * group, group)
                f_ref[out_rows, pl.ds(pl.multiple_of(i * chunk, 128), chunk)] = acc.astype(f_ref.dtype)
                return carry

            lax.fori_loop(0, block_len // chunk, chunk_body, 0)

    cols = (first_block + block) * block_len + lax.broadcasted_iota(jnp.int32, (1, block_len), 1)
    feats = jnp.where(cols < length - 1, f_ref[...], jnp.zeros_like(f_ref[...]))
    g_ref[...] += lax.dot_general(feats, feats, (((1,), (1,)), ((), ())), preferred_element_type=jnp.float32)
    c_ref[...] += lax.dot_general(tgt_ref[...], feats, (((1,), (1,)), ((), ())), preferred_element_type=jnp.float32)


def features_and_sums(window, base, first_block, n_blocks, depthwise_taps, target, top_dilation, length, interpret=False):
    channels = window.shape[0]
    dilations = dilation_list(top_dilation)
    n_filters, taps_per_filter = len(dilations), depthwise_taps.shape[1]
    span = (taps_per_filter - 1) * top_dilation
    rows = n_filters * channels
    block_len = min(TIME_BLOCK, length)
    taps = jnp.broadcast_to(
        depthwise_taps.reshape(n_filters * taps_per_filter, channels, 1),
        (n_filters * taps_per_filter, channels, 128),
    )
    kernel = functools.partial(feature_kernel, dilations, span, base, first_block, length, taps_per_filter)
    return pl.pallas_call(
        kernel,
        grid=(n_blocks,),
        in_specs=[
            pl.BlockSpec(memory_space=pltpu.VMEM),
            pl.BlockSpec(memory_space=pltpu.VMEM),
            pl.BlockSpec((1, block_len), lambda b: (0, b + first_block)),
        ],
        out_specs=[
            pl.BlockSpec((rows, block_len), lambda b: (0, b)),
            pl.BlockSpec((rows, rows), lambda b: (0, 0)),
            pl.BlockSpec((1, rows), lambda b: (0, 0)),
        ],
        out_shape=[
            jax.ShapeDtypeStruct((rows, n_blocks * block_len), jnp.bfloat16),
            jax.ShapeDtypeStruct((rows, rows), jnp.float32),
            jax.ShapeDtypeStruct((1, rows), jnp.float32),
        ],
        compiler_params=pltpu.CompilerParams(
            dimension_semantics=("arbitrary",), vmem_limit_bytes=48 * 1024 * 1024
        ),
        interpret=interpret,
    )(window, taps, target.reshape(1, length))


def solve_kernel(system_ref, c_ref, x_ref, a_ref, lt_ref):
    n = a_ref.shape[0]
    a_ref[...] = system_ref[...]
    lanes = lax.broadcasted_iota(jnp.int32, (1, n), 1)
    sublanes = lax.broadcasted_iota(jnp.int32, (n, 1), 0)

    def pick(vec, at):
        return jnp.sum(jnp.where(at, vec, 0.0), axis=1, keepdims=True)

    def factor_step(j, carry):
        rhs, forward, diag = carry
        at = lanes == j
        row = a_ref[pl.ds(j, 1), :]
        root = jnp.sqrt(pick(row, at))
        col_j = jnp.where(lanes >= j, row / root, 0.0)
        lt_ref[pl.ds(j, 1), :] = col_j
        yj = pick(rhs, at) / root
        rhs = rhs - yj * col_j
        forward = jnp.where(at, yj, forward)
        diag = jnp.where(at, root, diag)
        column = jnp.sum(jnp.where(lanes == j, a_ref[...], 0.0), axis=1, keepdims=True) / root
        column = jnp.where(sublanes >= j, column, 0.0)
        a_ref[...] = a_ref[...] - column * col_j
        return rhs, forward, diag

    zeros = jnp.zeros((1, n), jnp.float32)
    _, forward, diag = lax.fori_loop(0, n, factor_step, (c_ref[...], zeros, zeros))

    def back_step(t, x):
        j = n - 1 - t
        at = lanes == j
        partial = jnp.sum(lt_ref[pl.ds(j, 1), :] * x, axis=1, keepdims=True)
        return jnp.where(at, (pick(forward, at) - partial) / pick(diag, at), x)

    x_ref[...] = lax.fori_loop(0, n, back_step, zeros)


def ridge_solve_kernel(system, cross_sum, interpret=False):
    n = system.shape[0]
    return pl.pallas_call(
        solve_kernel,
        in_specs=[pl.BlockSpec(memory_space=pltpu.VMEM), pl.BlockSpec(memory_space=pltpu.VMEM)],
        out_specs=pl.BlockSpec(memory_space=pltpu.VMEM),
        out_shape=jax.ShapeDtypeStruct((1, n), jnp.float32),
        scratch_shapes=[pltpu.VMEM((n, n), jnp.float32), pltpu.VMEM((n, n), jnp.float32)],
        interpret=interpret,
    )(system, cross_sum.reshape(1, n))[0]


def jordan_kernel(system_ref, c_ref, x_ref, a_ref):
    n = a_ref.shape[0]
    a_ref[...] = system_ref[...]
    x_ref[...] = c_ref[...]
    sublanes = lax.broadcasted_iota(jnp.int32, (n, 1), 0)

    for lo in range(0, n, 128):
        lanes = lo + lax.broadcasted_iota(jnp.int32, (1, n - lo), 1)

        def step(j, carry, lo=lo, lanes=lanes):
            at = lanes == j
            here = sublanes == j
            row = a_ref[pl.ds(j, 1), :][:, lo:]
            pivot = jnp.sum(jnp.where(at, row, 0.0), axis=1, keepdims=True)
            column = jnp.sum(jnp.where(at, a_ref[:, lo:], 0.0), axis=1, keepdims=True)
            scaled_row = row / pivot
            scaled_rhs = x_ref[pl.ds(j, 1), :] / pivot
            a_ref[:, lo:] = jnp.where(here, scaled_row, a_ref[:, lo:] - column * scaled_row)
            x_ref[...] = jnp.where(here, scaled_rhs, x_ref[...] - column * scaled_rhs)
            return carry

        lax.fori_loop(lo, min(n, lo + 128), step, 0)


def ridge_solve_jordan(system, cross_sum, interpret=False):
    n = system.shape[0]
    rhs = jnp.broadcast_to(cross_sum[:, None], (n, 128))
    return pl.pallas_call(
        jordan_kernel,
        in_specs=[pl.BlockSpec(memory_space=pltpu.VMEM), pl.BlockSpec(memory_space=pltpu.VMEM)],
        out_specs=pl.BlockSpec(memory_space=pltpu.VMEM),
        out_shape=jax.ShapeDtypeStruct((n, 128), jnp.float32),
        scratch_shapes=[pltpu.VMEM((n, n), jnp.float32)],
        interpret=interpret,
    )(system, rhs)[:, 0]


def ridge_solve(system, cross_sum):
    factor = jnp.linalg.cholesky(system)
    middle = lax.linalg.triangular_solve(factor, cross_sum[:, None], left_side=True, lower=True)
    answer = lax.linalg.triangular_solve(
        factor, middle, left_side=True, lower=True, transpose_a=True
    )
    return answer[:, 0]


def butterfly_sum(x, axes):
    size = 1
    for name in axes:
        size *= lax.axis_size(name)
    if size & (size - 1):
        return lax.psum(x, axes)
    step = 1
    while step < size:
        x = x + lax.ppermute(x, axes, [(i, i ^ step) for i in range(size)])
        step *= 2
    return x


def reduce_system(gram_sum, cross_sum, axes):
    n = gram_sum.shape[0]
    h = n // 2
    rows = lax.broadcasted_iota(jnp.int32, (h, h), 0)
    cols = lax.broadcasted_iota(jnp.int32, (h, h), 1)
    lead, off, trail = gram_sum[:h, :h], gram_sum[:h, h:], gram_sum[h:, h:]
    folded = jnp.where(rows <= cols, lead, trail)
    extra = jnp.stack([cross_sum, jnp.concatenate([jnp.diagonal(trail), jnp.zeros((n - h,), jnp.float32)])])
    packed = jnp.concatenate([jnp.concatenate([folded, off], 1), extra], 0)
    packed = butterfly_sum(packed, axes)
    folded, off = packed[:h, :h], packed[:h, h:]
    upper = jnp.where(rows <= cols, folded, 0.0)
    lead = upper + jnp.where(rows < cols, folded, 0.0).T
    strict = jnp.where(rows > cols, folded, 0.0)
    trail = strict + strict.T + jnp.diag(packed[h + 1, :h])
    gram_sum = jnp.concatenate(
        [jnp.concatenate([lead, off], 1), jnp.concatenate([off.T, trail], 1)], 0
    )
    return gram_sum, packed[h]


def first_features(history, depthwise_taps, top_dilation):
    taps_per_filter = depthwise_taps.shape[1]
    last = history.shape[1] - 1
    samples = jnp.stack(
        [
            history[:, last - (taps_per_filter - 1) * d : last + 1 : d][:, ::-1]
            for d in dilation_list(top_dilation)
        ]
    )
    samples = jnp.transpose(samples, (0, 2, 1)).astype(jnp.float32)
    total = jnp.zeros(samples.shape[::2], jnp.float32)
    for k in range(taps_per_filter):
        total = total + depthwise_taps[:, k] * samples[:, k]
    return total.astype(jnp.bfloat16).reshape(-1)


def local(stream, target, depthwise_taps):
    length = stream.shape[1]
    top_dilation = min(1024, length // 16)
    history_len = 15 * top_dilation + 1
    span = history_len - 1
    sent = min(length, -(-history_len // 128) * 128)
    previous = shifted(stream[:, length - sent :], ("wide", "narrow"), 1)
    block_len = min(TIME_BLOCK, length)
    n_blocks = length // block_len
    split = min(n_blocks, -(-span // block_len))
    ahead = jnp.concatenate([target[1:], jnp.zeros_like(target[:1])])
    window = jnp.concatenate([previous[:, sent - span :], stream[:, : split * block_len]], 1)
    early, gram_sum, cross_sum = features_and_sums(
        window, 0, 0, split, depthwise_taps, ahead, top_dilation, length
    )
    parts = [early]
    if split < n_blocks:
        late, late_gram, late_cross = features_and_sums(
            stream, span, split, n_blocks - split, depthwise_taps, ahead, top_dilation, length
        )
        parts.append(late)
        gram_sum, cross_sum = gram_sum + late_gram, cross_sum + late_cross
    first = first_features(previous, depthwise_taps, top_dilation).astype(jnp.float32)
    gram_sum = gram_sum + first[:, None] * first[None, :]
    cross_sum = cross_sum[0] + first * target[0].astype(jnp.float32)
    gram_sum, cross_sum = reduce_system(gram_sum, cross_sum, ("wide", "narrow"))
    total_rows = length * lax.axis_size("wide") * lax.axis_size("narrow")
    system = gram_sum + ridge_share * total_rows * jnp.eye(gram_sum.shape[0], dtype=jnp.float32)
    coefficients = ridge_solve_jordan(system, cross_sum)
    rounded = coefficients.astype(jnp.bfloat16)
    fitted = [jnp.dot(rounded, first.astype(jnp.bfloat16), preferred_element_type=jnp.float32)[None]]
    fitted += [jnp.dot(rounded, f, preferred_element_type=jnp.float32) for f in parts]
    fitted = jnp.concatenate(fitted)[:length]
    return (coefficients, target.astype(jnp.float32) - fitted)


def solution(mesh):
    in_specs = (P(None, ("wide", "narrow")), P(("wide", "narrow")), P())
    out_specs = (P(), P(("wide", "narrow")))
    return jax.shard_map(local, mesh=mesh, in_specs=in_specs, out_specs=out_specs, check_vma=False)
```

```python
import functools

import jax
import jax.numpy as jnp
from jax import lax
from jax.sharding import PartitionSpec as P
from jax.experimental import pallas as pl
from jax.experimental.pallas import tpu as pltpu

ridge_share = 0.05


def shifted(array, axis, by):
    size = lax.axis_size(axis)
    pairs = [(i, i + by) for i in range(size) if 0 <= i + by < size]
    return lax.ppermute(array, axis, pairs)


def dilation_list(top_dilation):
    return (1, top_dilation // 16, top_dilation // 4, top_dilation)


def filter_bank(window, depthwise_taps, top_dilation, history_len, length):
    row_list = []
    for j, d in enumerate(dilation_list(top_dilation)):
        total = jnp.zeros((window.shape[0], length), jnp.float32)
        for k in range(depthwise_taps.shape[1]):
            start_offset = history_len - 1 - k * d
            total = (
                total
                + depthwise_taps[j, k][:, None] * window[:, start_offset : start_offset + length]
            )
        row_list.append(total.astype(jnp.bfloat16))
    return jnp.concatenate(row_list, 0)


TIME_BLOCK = 2048
ROW_GROUP = 16
NARROW_CHUNK = 1024
WIDE_CHUNK = 1024


def feature_kernel(dilations, span, base, first_block, taps_per_filter, w_ref, taps_ref, tgt_ref, f_ref, g_ref, c_ref):
    block = pl.program_id(0)
    block_len = f_ref.shape[1]
    channels = w_ref.shape[0]
    group = ROW_GROUP

    @pl.when(block == 0)
    def _():
        g_ref[...] = jnp.zeros_like(g_ref)
        c_ref[...] = jnp.zeros_like(c_ref)

    for j, d in enumerate(dilations):
        chunk = min(block_len, NARROW_CHUNK if d % 64 else WIDE_CHUNK)
        for g in range(channels // group):
            rows = pl.ds(g * group, group)

            def chunk_body(i, carry, j=j, d=d, rows=rows, g=g, chunk=chunk):
                start = pl.multiple_of((first_block + block) * block_len + i * chunk, 128)
                slabs = {}
                acc = None
                for k in range(taps_per_filter):
                    offset = span - k * d - base
                    r = offset % 128
                    a = offset - r
                    if r == 0:
                        x = w_ref[rows, pl.ds(pl.multiple_of(start + a, 128), chunk)].astype(jnp.float32)
                    else:
                        if a not in slabs:
                            slabs[a] = w_ref[rows, pl.ds(pl.multiple_of(start + a, 128), chunk + 128)].astype(jnp.float32)
                        x = slabs[a][:, r:r + chunk]
                    w = jnp.tile(taps_ref[j * taps_per_filter + k, rows, :], (1, chunk // 128))
                    acc = w * x if acc is None else acc + w * x
                out_rows = pl.ds(j * channels + g * group, group)
                f_ref[out_rows, pl.ds(pl.multiple_of(i * chunk, 128), chunk)] = acc.astype(f_ref.dtype)
                return carry

            lax.fori_loop(0, block_len // chunk, chunk_body, 0)

    feats = f_ref[...]
    g_ref[...] += lax.dot_general(feats, feats, (((1,), (1,)), ((), ())), preferred_element_type=jnp.float32)
    c_ref[...] += lax.dot_general(tgt_ref[...], feats, (((1,), (1,)), ((), ())), preferred_element_type=jnp.float32)


def features_and_sums(window, base, first_block, n_blocks, depthwise_taps, target, top_dilation, length, interpret=False):
    channels = window.shape[0]
    dilations = dilation_list(top_dilation)
    n_filters, taps_per_filter = len(dilations), depthwise_taps.shape[1]
    span = (taps_per_filter - 1) * top_dilation
    rows = n_filters * channels
    block_len = min(TIME_BLOCK, length)
    taps = jnp.broadcast_to(
        depthwise_taps.reshape(n_filters * taps_per_filter, channels, 1),
        (n_filters * taps_per_filter, channels, 128),
    )
    kernel = functools.partial(feature_kernel, dilations, span, base, first_block, taps_per_filter)
    return pl.pallas_call(
        kernel,
        grid=(n_blocks,),
        in_specs=[
            pl.BlockSpec(memory_space=pltpu.VMEM),
            pl.BlockSpec(memory_space=pltpu.VMEM),
            pl.BlockSpec((1, block_len), lambda b: (0, b + first_block)),
        ],
        out_specs=[
            pl.BlockSpec((rows, block_len), lambda b: (0, b)),
            pl.BlockSpec((rows, rows), lambda b: (0, 0)),
            pl.BlockSpec((1, rows), lambda b: (0, 0)),
        ],
        out_shape=[
            jax.ShapeDtypeStruct((rows, n_blocks * block_len), jnp.bfloat16),
            jax.ShapeDtypeStruct((rows, rows), jnp.float32),
            jax.ShapeDtypeStruct((1, rows), jnp.float32),
        ],
        compiler_params=pltpu.CompilerParams(
            dimension_semantics=("arbitrary",), vmem_limit_bytes=48 * 1024 * 1024
        ),
        interpret=interpret,
    )(window, taps, target.reshape(1, length))


def solve_kernel(system_ref, c_ref, x_ref, a_ref, lt_ref):
    n = a_ref.shape[0]
    a_ref[...] = system_ref[...]
    lanes = lax.broadcasted_iota(jnp.int32, (1, n), 1)
    sublanes = lax.broadcasted_iota(jnp.int32, (n, 1), 0)

    def pick(vec, at):
        return jnp.sum(jnp.where(at, vec, 0.0), axis=1, keepdims=True)

    def factor_step(j, carry):
        rhs, forward, diag = carry
        at = lanes == j
        row = a_ref[pl.ds(j, 1), :]
        root = jnp.sqrt(pick(row, at))
        col_j = jnp.where(lanes >= j, row / root, 0.0)
        lt_ref[pl.ds(j, 1), :] = col_j
        yj = pick(rhs, at) / root
        rhs = rhs - yj * col_j
        forward = jnp.where(at, yj, forward)
        diag = jnp.where(at, root, diag)
        column = jnp.sum(jnp.where(lanes == j, a_ref[...], 0.0), axis=1, keepdims=True) / root
        column = jnp.where(sublanes >= j, column, 0.0)
        a_ref[...] = a_ref[...] - column * col_j
        return rhs, forward, diag

    zeros = jnp.zeros((1, n), jnp.float32)
    _, forward, diag = lax.fori_loop(0, n, factor_step, (c_ref[...], zeros, zeros))

    def back_step(t, x):
        j = n - 1 - t
        at = lanes == j
        partial = jnp.sum(lt_ref[pl.ds(j, 1), :] * x, axis=1, keepdims=True)
        return jnp.where(at, (pick(forward, at) - partial) / pick(diag, at), x)

    x_ref[...] = lax.fori_loop(0, n, back_step, zeros)


def ridge_solve_kernel(system, cross_sum, interpret=False):
    n = system.shape[0]
    return pl.pallas_call(
        solve_kernel,
        in_specs=[pl.BlockSpec(memory_space=pltpu.VMEM), pl.BlockSpec(memory_space=pltpu.VMEM)],
        out_specs=pl.BlockSpec(memory_space=pltpu.VMEM),
        out_shape=jax.ShapeDtypeStruct((1, n), jnp.float32),
        scratch_shapes=[pltpu.VMEM((n, n), jnp.float32), pltpu.VMEM((n, n), jnp.float32)],
        interpret=interpret,
    )(system, cross_sum.reshape(1, n))[0]


def jordan_kernel(system_ref, c_ref, x_ref, a_ref):
    n = a_ref.shape[0]
    a_ref[...] = system_ref[...]
    x_ref[...] = c_ref[...]
    sublanes = lax.broadcasted_iota(jnp.int32, (n, 1), 0)

    for lo in range(0, n, 128):
        lanes = lo + lax.broadcasted_iota(jnp.int32, (1, n - lo), 1)

        def step(j, carry, lo=lo, lanes=lanes):
            at = lanes == j
            here = sublanes == j
            row = a_ref[pl.ds(j, 1), :][:, lo:]
            pivot = jnp.sum(jnp.where(at, row, 0.0), axis=1, keepdims=True)
            column = jnp.sum(jnp.where(at, a_ref[:, lo:], 0.0), axis=1, keepdims=True)
            scaled_row = row / pivot
            scaled_rhs = x_ref[pl.ds(j, 1), :] / pivot
            a_ref[:, lo:] = jnp.where(here, scaled_row, a_ref[:, lo:] - column * scaled_row)
            x_ref[...] = jnp.where(here, scaled_rhs, x_ref[...] - column * scaled_rhs)
            return carry

        lax.fori_loop(lo, min(n, lo + 128), step, 0)


def ridge_solve_jordan(system, cross_sum, interpret=False):
    n = system.shape[0]
    rhs = jnp.broadcast_to(cross_sum[:, None], (n, 128))
    return pl.pallas_call(
        jordan_kernel,
        in_specs=[pl.BlockSpec(memory_space=pltpu.VMEM), pl.BlockSpec(memory_space=pltpu.VMEM)],
        out_specs=pl.BlockSpec(memory_space=pltpu.VMEM),
        out_shape=jax.ShapeDtypeStruct((n, 128), jnp.float32),
        scratch_shapes=[pltpu.VMEM((n, n), jnp.float32)],
        interpret=interpret,
    )(system, rhs)[:, 0]


def ridge_solve(system, cross_sum):
    factor = jnp.linalg.cholesky(system)
    middle = lax.linalg.triangular_solve(factor, cross_sum[:, None], left_side=True, lower=True)
    answer = lax.linalg.triangular_solve(
        factor, middle, left_side=True, lower=True, transpose_a=True
    )
    return answer[:, 0]


def butterfly_sum(x, axes):
    size = 1
    for name in axes:
        size *= lax.axis_size(name)
    if size & (size - 1):
        return lax.psum(x, axes)
    step = 1
    while step < size:
        x = x + lax.ppermute(x, axes, [(i, i ^ step) for i in range(size)])
        step *= 2
    return x


def reduce_system(gram_sum, cross_sum, axes):
    n = gram_sum.shape[0]
    h = n // 2
    rows = lax.broadcasted_iota(jnp.int32, (h, h), 0)
    cols = lax.broadcasted_iota(jnp.int32, (h, h), 1)
    lead, off, trail = gram_sum[:h, :h], gram_sum[:h, h:], gram_sum[h:, h:]
    folded = jnp.where(rows <= cols, lead, trail)
    extra = jnp.stack([cross_sum, jnp.concatenate([jnp.diagonal(trail), jnp.zeros((n - h,), jnp.float32)])])
    packed = jnp.concatenate([jnp.concatenate([folded, off], 1), extra], 0)
    packed = butterfly_sum(packed, axes)
    folded, off = packed[:h, :h], packed[:h, h:]
    upper = jnp.where(rows <= cols, folded, 0.0)
    lead = upper + jnp.where(rows < cols, folded, 0.0).T
    strict = jnp.where(rows > cols, folded, 0.0)
    trail = strict + strict.T + jnp.diag(packed[h + 1, :h])
    gram_sum = jnp.concatenate(
        [jnp.concatenate([lead, off], 1), jnp.concatenate([off.T, trail], 1)], 0
    )
    return gram_sum, packed[h]


def local(stream, target, depthwise_taps):
    length = stream.shape[1]
    top_dilation = min(1024, length // 16)
    history_len = 15 * top_dilation + 1
    tail_end = stream[:, length - history_len :]
    previous = shifted(tail_end, ("wide", "narrow"), 1)
    span = history_len - 1
    block_len = min(TIME_BLOCK, length)
    n_blocks = length // block_len
    split = min(n_blocks, -(-span // block_len))
    window = jnp.concatenate([previous, stream], 1)[:, : split * block_len + span]
    features, gram_sum, cross_sum = features_and_sums(
        window, 0, 0, split, depthwise_taps, target, top_dilation, length
    )
    if split < n_blocks:
        delayed = jnp.concatenate([jnp.zeros_like(stream[:, :1]), stream[:, : length - 1]], 1)
        late_features, late_gram, late_cross = features_and_sums(
            delayed, span, split, n_blocks - split, depthwise_taps, target, top_dilation, length
        )
        features = (features, late_features)
        gram_sum, cross_sum = gram_sum + late_gram, cross_sum + late_cross
    else:
        features = (features,)
    cross_sum = cross_sum[0]
    gram_sum, cross_sum = reduce_system(gram_sum, cross_sum, ("wide", "narrow"))
    total_rows = length * lax.axis_size("wide") * lax.axis_size("narrow")
    system = gram_sum + ridge_share * total_rows * jnp.eye(gram_sum.shape[0], dtype=jnp.float32)
    coefficients = ridge_solve_jordan(system, cross_sum)
    rounded = coefficients.astype(jnp.bfloat16)
    fitted = jnp.concatenate([jnp.dot(rounded, f, preferred_element_type=jnp.float32) for f in features])
    return (coefficients, target.astype(jnp.float32) - fitted)


def solution(mesh):
    in_specs = (P(None, ("wide", "narrow")), P(("wide", "narrow")), P())
    out_specs = (P(), P(("wide", "narrow")))
    return jax.shard_map(local, mesh=mesh, in_specs=in_specs, out_specs=out_specs, check_vma=False)
```

```python
import functools

import jax
import jax.numpy as jnp
from jax import lax
from jax.sharding import PartitionSpec as P
from jax.experimental import pallas as pl
from jax.experimental.pallas import tpu as pltpu

ridge_share = 0.05


def shifted(array, axis, by):
    size = lax.axis_size(axis)
    pairs = [(i, i + by) for i in range(size) if 0 <= i + by < size]
    return lax.ppermute(array, axis, pairs)


def dilation_list(top_dilation):
    return (1, top_dilation // 16, top_dilation // 4, top_dilation)


def filter_bank(window, depthwise_taps, top_dilation, history_len, length):
    row_list = []
    for j, d in enumerate(dilation_list(top_dilation)):
        total = jnp.zeros((window.shape[0], length), jnp.float32)
        for k in range(depthwise_taps.shape[1]):
            start_offset = history_len - 1 - k * d
            total = (
                total
                + depthwise_taps[j, k][:, None] * window[:, start_offset : start_offset + length]
            )
        row_list.append(total.astype(jnp.bfloat16))
    return jnp.concatenate(row_list, 0)


TIME_BLOCK = 2048
ROW_GROUP = 16
NARROW_CHUNK = 1024
WIDE_CHUNK = 1024


def feature_kernel(dilations, span, base, first_block, taps_per_filter, w_ref, taps_ref, tgt_ref, f_ref, g_ref, c_ref):
    block = pl.program_id(0)
    block_len = f_ref.shape[1]
    channels = w_ref.shape[0]
    group = ROW_GROUP

    @pl.when(block == 0)
    def _():
        g_ref[...] = jnp.zeros_like(g_ref)
        c_ref[...] = jnp.zeros_like(c_ref)

    for j, d in enumerate(dilations):
        chunk = min(block_len, NARROW_CHUNK if d % 64 else WIDE_CHUNK)
        for g in range(channels // group):
            rows = pl.ds(g * group, group)

            def chunk_body(i, carry, j=j, d=d, rows=rows, g=g, chunk=chunk):
                start = pl.multiple_of((first_block + block) * block_len + i * chunk, 128)
                slabs = {}
                acc = None
                for k in range(taps_per_filter):
                    offset = span - k * d - base
                    r = offset % 128
                    a = offset - r
                    if r == 0:
                        x = w_ref[rows, pl.ds(pl.multiple_of(start + a, 128), chunk)].astype(jnp.float32)
                    else:
                        if a not in slabs:
                            slabs[a] = w_ref[rows, pl.ds(pl.multiple_of(start + a, 128), chunk + 128)].astype(jnp.float32)
                        x = slabs[a][:, r:r + chunk]
                    w = jnp.tile(taps_ref[j * taps_per_filter + k, rows, :], (1, chunk // 128))
                    acc = w * x if acc is None else acc + w * x
                out_rows = pl.ds(j * channels + g * group, group)
                f_ref[out_rows, pl.ds(pl.multiple_of(i * chunk, 128), chunk)] = acc.astype(f_ref.dtype)
                return carry

            lax.fori_loop(0, block_len // chunk, chunk_body, 0)

    feats = f_ref[...]
    g_ref[...] += lax.dot_general(feats, feats, (((1,), (1,)), ((), ())), preferred_element_type=jnp.float32)
    c_ref[...] += lax.dot_general(tgt_ref[...], feats, (((1,), (1,)), ((), ())), preferred_element_type=jnp.float32)


def features_and_sums(window, base, first_block, n_blocks, depthwise_taps, target, top_dilation, length, interpret=False):
    channels = window.shape[0]
    dilations = dilation_list(top_dilation)
    n_filters, taps_per_filter = len(dilations), depthwise_taps.shape[1]
    span = (taps_per_filter - 1) * top_dilation
    rows = n_filters * channels
    block_len = min(TIME_BLOCK, length)
    taps = jnp.broadcast_to(
        depthwise_taps.reshape(n_filters * taps_per_filter, channels, 1),
        (n_filters * taps_per_filter, channels, 128),
    )
    kernel = functools.partial(feature_kernel, dilations, span, base, first_block, taps_per_filter)
    return pl.pallas_call(
        kernel,
        grid=(n_blocks,),
        in_specs=[
            pl.BlockSpec(memory_space=pltpu.VMEM),
            pl.BlockSpec(memory_space=pltpu.VMEM),
            pl.BlockSpec((1, block_len), lambda b: (0, b + first_block)),
        ],
        out_specs=[
            pl.BlockSpec((rows, block_len), lambda b: (0, b)),
            pl.BlockSpec((rows, rows), lambda b: (0, 0)),
            pl.BlockSpec((1, rows), lambda b: (0, 0)),
        ],
        out_shape=[
            jax.ShapeDtypeStruct((rows, n_blocks * block_len), jnp.bfloat16),
            jax.ShapeDtypeStruct((rows, rows), jnp.float32),
            jax.ShapeDtypeStruct((1, rows), jnp.float32),
        ],
        compiler_params=pltpu.CompilerParams(
            dimension_semantics=("arbitrary",), vmem_limit_bytes=48 * 1024 * 1024
        ),
        interpret=interpret,
    )(window, taps, target.reshape(1, length))


def solve_kernel(system_ref, c_ref, x_ref, a_ref, lt_ref):
    n = a_ref.shape[0]
    a_ref[...] = system_ref[...]
    lanes = lax.broadcasted_iota(jnp.int32, (1, n), 1)
    sublanes = lax.broadcasted_iota(jnp.int32, (n, 1), 0)

    def pick(vec, at):
        return jnp.sum(jnp.where(at, vec, 0.0), axis=1, keepdims=True)

    def factor_step(j, carry):
        rhs, forward, diag = carry
        at = lanes == j
        row = a_ref[pl.ds(j, 1), :]
        root = jnp.sqrt(pick(row, at))
        col_j = jnp.where(lanes >= j, row / root, 0.0)
        lt_ref[pl.ds(j, 1), :] = col_j
        yj = pick(rhs, at) / root
        rhs = rhs - yj * col_j
        forward = jnp.where(at, yj, forward)
        diag = jnp.where(at, root, diag)
        column = jnp.sum(jnp.where(lanes == j, a_ref[...], 0.0), axis=1, keepdims=True) / root
        column = jnp.where(sublanes >= j, column, 0.0)
        a_ref[...] = a_ref[...] - column * col_j
        return rhs, forward, diag

    zeros = jnp.zeros((1, n), jnp.float32)
    _, forward, diag = lax.fori_loop(0, n, factor_step, (c_ref[...], zeros, zeros))

    def back_step(t, x):
        j = n - 1 - t
        at = lanes == j
        partial = jnp.sum(lt_ref[pl.ds(j, 1), :] * x, axis=1, keepdims=True)
        return jnp.where(at, (pick(forward, at) - partial) / pick(diag, at), x)

    x_ref[...] = lax.fori_loop(0, n, back_step, zeros)


def ridge_solve_kernel(system, cross_sum, interpret=False):
    n = system.shape[0]
    return pl.pallas_call(
        solve_kernel,
        in_specs=[pl.BlockSpec(memory_space=pltpu.VMEM), pl.BlockSpec(memory_space=pltpu.VMEM)],
        out_specs=pl.BlockSpec(memory_space=pltpu.VMEM),
        out_shape=jax.ShapeDtypeStruct((1, n), jnp.float32),
        scratch_shapes=[pltpu.VMEM((n, n), jnp.float32), pltpu.VMEM((n, n), jnp.float32)],
        interpret=interpret,
    )(system, cross_sum.reshape(1, n))[0]


def jordan_kernel(ridge, packed_ref, x_ref, a_ref):
    n = a_ref.shape[0]
    h = n // 2
    rows = lax.broadcasted_iota(jnp.int32, (h, h), 0)
    cols = lax.broadcasted_iota(jnp.int32, (h, h), 1)
    folded = packed_ref[:h, :h]
    flipped = jnp.transpose(folded)
    off = packed_ref[:h, h:]
    trail_diag = packed_ref[h + 1 : h + 2, :h]
    a_ref[:h, :h] = jnp.where(rows <= cols, folded, flipped) + jnp.where(rows == cols, ridge, 0.0)
    a_ref[:h, h:] = off
    a_ref[h:, :h] = jnp.transpose(off)
    a_ref[h:, h:] = jnp.where(rows > cols, folded, jnp.where(rows < cols, flipped, trail_diag + ridge))
    x_ref[...] = jnp.transpose(jnp.broadcast_to(packed_ref[h : h + 1, :], (128, n)))
    sublanes = lax.broadcasted_iota(jnp.int32, (n, 1), 0)

    for lo in range(0, n, 128):
        lanes = lo + lax.broadcasted_iota(jnp.int32, (1, n - lo), 1)

        def step(j, carry, lo=lo, lanes=lanes):
            at = lanes == j
            here = sublanes == j
            row = a_ref[pl.ds(j, 1), :][:, lo:]
            pivot = jnp.sum(jnp.where(at, row, 0.0), axis=1, keepdims=True)
            column = jnp.sum(jnp.where(at, a_ref[:, lo:], 0.0), axis=1, keepdims=True)
            scaled_row = row / pivot
            scaled_rhs = x_ref[pl.ds(j, 1), :] / pivot
            a_ref[:, lo:] = jnp.where(here, scaled_row, a_ref[:, lo:] - column * scaled_row)
            x_ref[...] = jnp.where(here, scaled_rhs, x_ref[...] - column * scaled_rhs)
            return carry

        lax.fori_loop(lo, min(n, lo + 128), step, 0)


def ridge_solve_packed(packed, ridge, interpret=False):
    n = packed.shape[1]
    return pl.pallas_call(
        functools.partial(jordan_kernel, ridge),
        in_specs=[pl.BlockSpec(memory_space=pltpu.VMEM)],
        out_specs=pl.BlockSpec(memory_space=pltpu.VMEM),
        out_shape=jax.ShapeDtypeStruct((n, 128), jnp.float32),
        scratch_shapes=[pltpu.VMEM((n, n), jnp.float32)],
        interpret=interpret,
    )(packed)[:, 0]


def ridge_solve(system, cross_sum):
    factor = jnp.linalg.cholesky(system)
    middle = lax.linalg.triangular_solve(factor, cross_sum[:, None], left_side=True, lower=True)
    answer = lax.linalg.triangular_solve(
        factor, middle, left_side=True, lower=True, transpose_a=True
    )
    return answer[:, 0]


def butterfly_sum(x, axes):
    size = 1
    for name in axes:
        size *= lax.axis_size(name)
    if size & (size - 1):
        return lax.psum(x, axes)
    step = 1
    while step < size:
        x = x + lax.ppermute(x, axes, [(i, i ^ step) for i in range(size)])
        step *= 2
    return x


def reduce_system(gram_sum, cross_sum, axes):
    n = gram_sum.shape[0]
    h = n // 2
    rows = lax.broadcasted_iota(jnp.int32, (h, h), 0)
    cols = lax.broadcasted_iota(jnp.int32, (h, h), 1)
    lead, off, trail = gram_sum[:h, :h], gram_sum[:h, h:], gram_sum[h:, h:]
    folded = jnp.where(rows <= cols, lead, trail)
    extra = jnp.stack([cross_sum, jnp.concatenate([jnp.diagonal(trail), jnp.zeros((n - h,), jnp.float32)])])
    packed = jnp.concatenate([jnp.concatenate([folded, off], 1), extra], 0)
    return butterfly_sum(packed, axes)


def local(stream, target, depthwise_taps):
    length = stream.shape[1]
    top_dilation = min(1024, length // 16)
    history_len = 15 * top_dilation + 1
    tail_end = stream[:, length - history_len :]
    previous = shifted(tail_end, ("wide", "narrow"), 1)
    span = history_len - 1
    block_len = min(TIME_BLOCK, length)
    n_blocks = length // block_len
    split = min(n_blocks, -(-span // block_len))
    window = jnp.concatenate([previous, stream], 1)[:, : split * block_len + span]
    features, gram_sum, cross_sum = features_and_sums(
        window, 0, 0, split, depthwise_taps, target, top_dilation, length
    )
    if split < n_blocks:
        delayed = jnp.concatenate([jnp.zeros_like(stream[:, :1]), stream[:, : length - 1]], 1)
        late_features, late_gram, late_cross = features_and_sums(
            delayed, span, split, n_blocks - split, depthwise_taps, target, top_dilation, length
        )
        features = (features, late_features)
        gram_sum, cross_sum = gram_sum + late_gram, cross_sum + late_cross
    else:
        features = (features,)
    cross_sum = cross_sum[0]
    packed = reduce_system(gram_sum, cross_sum, ("wide", "narrow"))
    total_rows = length * lax.axis_size("wide") * lax.axis_size("narrow")
    coefficients = ridge_solve_packed(packed, ridge_share * total_rows)
    rounded = coefficients.astype(jnp.bfloat16)
    fitted = jnp.concatenate([jnp.dot(rounded, f, preferred_element_type=jnp.float32) for f in features])
    return (coefficients, target.astype(jnp.float32) - fitted)


def solution(mesh):
    in_specs = (P(None, ("wide", "narrow")), P(("wide", "narrow")), P())
    out_specs = (P(), P(("wide", "narrow")))
    return jax.shard_map(local, mesh=mesh, in_specs=in_specs, out_specs=out_specs, check_vma=False)
```

```python
import functools

import jax
import jax.numpy as jnp
from jax import lax
from jax.sharding import PartitionSpec as P
from jax.experimental import pallas as pl
from jax.experimental.pallas import tpu as pltpu

ridge_share = 0.05


def shifted(array, axis, by):
    size = lax.axis_size(axis)
    pairs = [(i, i + by) for i in range(size) if 0 <= i + by < size]
    return lax.ppermute(array, axis, pairs)


def dilation_list(top_dilation):
    return (1, top_dilation // 16, top_dilation // 4, top_dilation)


def filter_bank(window, depthwise_taps, top_dilation, history_len, length):
    row_list = []
    for j, d in enumerate(dilation_list(top_dilation)):
        total = jnp.zeros((window.shape[0], length), jnp.float32)
        for k in range(depthwise_taps.shape[1]):
            start_offset = history_len - 1 - k * d
            total = (
                total
                + depthwise_taps[j, k][:, None] * window[:, start_offset : start_offset + length]
            )
        row_list.append(total.astype(jnp.bfloat16))
    return jnp.concatenate(row_list, 0)


TIME_BLOCK = 2048
ROW_GROUP = 16
NARROW_CHUNK = 1024
WIDE_CHUNK = 1024


def feature_kernel(dilations, span, base, first_block, taps_per_filter, w_ref, taps_ref, tgt_ref, f_ref, g_ref, c_ref):
    block = pl.program_id(0)
    block_len = f_ref.shape[1]
    channels = w_ref.shape[0]
    group = ROW_GROUP

    @pl.when(block == 0)
    def _():
        g_ref[...] = jnp.zeros_like(g_ref)
        c_ref[...] = jnp.zeros_like(c_ref)

    for j, d in enumerate(dilations):
        chunk = min(block_len, NARROW_CHUNK if d % 64 else WIDE_CHUNK)
        for g in range(channels // group):
            rows = pl.ds(g * group, group)

            def chunk_body(i, carry, j=j, d=d, rows=rows, g=g, chunk=chunk):
                start = pl.multiple_of((first_block + block) * block_len + i * chunk, 128)
                slabs = {}
                acc = None
                for k in range(taps_per_filter):
                    offset = span - k * d - base
                    r = offset % 128
                    a = offset - r
                    if r == 0:
                        x = w_ref[rows, pl.ds(pl.multiple_of(start + a, 128), chunk)].astype(jnp.float32)
                    else:
                        if a not in slabs:
                            slabs[a] = w_ref[rows, pl.ds(pl.multiple_of(start + a, 128), chunk + 128)].astype(jnp.float32)
                        x = slabs[a][:, r:r + chunk]
                    w = jnp.tile(taps_ref[j * taps_per_filter + k, rows, :], (1, chunk // 128))
                    acc = w * x if acc is None else acc + w * x
                out_rows = pl.ds(j * channels + g * group, group)
                f_ref[out_rows, pl.ds(pl.multiple_of(i * chunk, 128), chunk)] = acc.astype(f_ref.dtype)
                return carry

            lax.fori_loop(0, block_len // chunk, chunk_body, 0)

    feats = f_ref[...]
    g_ref[...] += lax.dot_general(feats, feats, (((1,), (1,)), ((), ())), preferred_element_type=jnp.float32)
    c_ref[...] += lax.dot_general(tgt_ref[...], feats, (((1,), (1,)), ((), ())), preferred_element_type=jnp.float32)


def features_and_sums(window, base, first_block, n_blocks, depthwise_taps, target, top_dilation, length, interpret=False):
    channels = window.shape[0]
    dilations = dilation_list(top_dilation)
    n_filters, taps_per_filter = len(dilations), depthwise_taps.shape[1]
    span = (taps_per_filter - 1) * top_dilation
    rows = n_filters * channels
    block_len = min(TIME_BLOCK, length)
    taps = jnp.broadcast_to(
        depthwise_taps.reshape(n_filters * taps_per_filter, channels, 1),
        (n_filters * taps_per_filter, channels, 128),
    )
    kernel = functools.partial(feature_kernel, dilations, span, base, first_block, taps_per_filter)
    return pl.pallas_call(
        kernel,
        grid=(n_blocks,),
        in_specs=[
            pl.BlockSpec(memory_space=pltpu.VMEM),
            pl.BlockSpec(memory_space=pltpu.VMEM),
            pl.BlockSpec((1, block_len), lambda b: (0, b + first_block)),
        ],
        out_specs=[
            pl.BlockSpec((rows, block_len), lambda b: (0, b)),
            pl.BlockSpec((rows, rows), lambda b: (0, 0)),
            pl.BlockSpec((1, rows), lambda b: (0, 0)),
        ],
        out_shape=[
            jax.ShapeDtypeStruct((rows, n_blocks * block_len), jnp.bfloat16),
            jax.ShapeDtypeStruct((rows, rows), jnp.float32),
            jax.ShapeDtypeStruct((1, rows), jnp.float32),
        ],
        compiler_params=pltpu.CompilerParams(
            dimension_semantics=("arbitrary",), vmem_limit_bytes=48 * 1024 * 1024
        ),
        interpret=interpret,
    )(window, taps, target.reshape(1, length))


def solve_kernel(system_ref, c_ref, x_ref, a_ref, lt_ref):
    n = a_ref.shape[0]
    a_ref[...] = system_ref[...]
    lanes = lax.broadcasted_iota(jnp.int32, (1, n), 1)
    sublanes = lax.broadcasted_iota(jnp.int32, (n, 1), 0)

    def pick(vec, at):
        return jnp.sum(jnp.where(at, vec, 0.0), axis=1, keepdims=True)

    def factor_step(j, carry):
        rhs, forward, diag = carry
        at = lanes == j
        row = a_ref[pl.ds(j, 1), :]
        root = jnp.sqrt(pick(row, at))
        col_j = jnp.where(lanes >= j, row / root, 0.0)
        lt_ref[pl.ds(j, 1), :] = col_j
        yj = pick(rhs, at) / root
        rhs = rhs - yj * col_j
        forward = jnp.where(at, yj, forward)
        diag = jnp.where(at, root, diag)
        column = jnp.sum(jnp.where(lanes == j, a_ref[...], 0.0), axis=1, keepdims=True) / root
        column = jnp.where(sublanes >= j, column, 0.0)
        a_ref[...] = a_ref[...] - column * col_j
        return rhs, forward, diag

    zeros = jnp.zeros((1, n), jnp.float32)
    _, forward, diag = lax.fori_loop(0, n, factor_step, (c_ref[...], zeros, zeros))

    def back_step(t, x):
        j = n - 1 - t
        at = lanes == j
        partial = jnp.sum(lt_ref[pl.ds(j, 1), :] * x, axis=1, keepdims=True)
        return jnp.where(at, (pick(forward, at) - partial) / pick(diag, at), x)

    x_ref[...] = lax.fori_loop(0, n, back_step, zeros)


def ridge_solve_kernel(system, cross_sum, interpret=False):
    n = system.shape[0]
    return pl.pallas_call(
        solve_kernel,
        in_specs=[pl.BlockSpec(memory_space=pltpu.VMEM), pl.BlockSpec(memory_space=pltpu.VMEM)],
        out_specs=pl.BlockSpec(memory_space=pltpu.VMEM),
        out_shape=jax.ShapeDtypeStruct((1, n), jnp.float32),
        scratch_shapes=[pltpu.VMEM((n, n), jnp.float32), pltpu.VMEM((n, n), jnp.float32)],
        interpret=interpret,
    )(system, cross_sum.reshape(1, n))[0]


def jordan_kernel(ridge, packed_ref, x_ref, a_ref):
    n = a_ref.shape[0]
    h = n // 2
    rows = lax.broadcasted_iota(jnp.int32, (h, h), 0)
    cols = lax.broadcasted_iota(jnp.int32, (h, h), 1)
    folded = packed_ref[:h, :h]
    flipped = jnp.transpose(folded)
    off = packed_ref[:h, h:]
    trail_diag = packed_ref[h + 1 : h + 2, :h]
    a_ref[:h, :h] = jnp.where(rows <= cols, folded, flipped) + jnp.where(rows == cols, ridge, 0.0)
    a_ref[:h, h:] = off
    a_ref[h:, :h] = jnp.transpose(off)
    a_ref[h:, h:] = jnp.where(rows > cols, folded, jnp.where(rows < cols, flipped, trail_diag + ridge))
    x_ref[...] = jnp.transpose(jnp.broadcast_to(packed_ref[h : h + 1, :], (128, n)))
    sublanes = lax.broadcasted_iota(jnp.int32, (n, 1), 0)

    for lo in range(0, n, 128):
        lanes = lo + lax.broadcasted_iota(jnp.int32, (1, n - lo), 1)

        def pick(vec, at):
            return jnp.sum(jnp.where(at, vec, 0.0), axis=1, keepdims=True)

        def step(p, carry, lo=lo, lanes=lanes):
            j = 2 * p
            at0, at1 = lanes == j, lanes == j + 1
            here0, here1 = sublanes == j, sublanes == j + 1
            block = a_ref[:, lo:]
            row0 = a_ref[pl.ds(j, 1), :][:, lo:]
            row1 = a_ref[pl.ds(j + 1, 1), :][:, lo:]
            col0 = jnp.sum(jnp.where(at0, block, 0.0), axis=1, keepdims=True)
            col1 = jnp.sum(jnp.where(at1, block, 0.0), axis=1, keepdims=True)
            rhs0 = x_ref[pl.ds(j, 1), :]
            rhs1 = x_ref[pl.ds(j + 1, 1), :]
            pivot0 = pick(row0, at0)
            srow0 = row0 / pivot0
            srhs0 = rhs0 / pivot0
            lower = pick(row1, at0)
            row1 = row1 - lower * srow0
            rhs1 = rhs1 - lower * srhs0
            upper = pick(srow0, at1)
            col1 = jnp.where(here0, upper, col1 - col0 * upper)
            pivot1 = pick(row1, at1)
            srow1 = row1 / pivot1
            srhs1 = rhs1 / pivot1
            rest = block - col0 * srow0 - col1 * srow1
            done0 = srow0 - upper * srow1
            a_ref[:, lo:] = jnp.where(here1, srow1, jnp.where(here0, done0, rest))
            x = x_ref[...]
            x_rest = x - col0 * srhs0 - col1 * srhs1
            x_ref[...] = jnp.where(here1, srhs1, jnp.where(here0, srhs0 - upper * srhs1, x_rest))
            return carry

        lax.fori_loop(lo // 2, min(n, lo + 128) // 2, step, 0)


def ridge_solve_packed(packed, ridge, interpret=False):
    n = packed.shape[1]
    return pl.pallas_call(
        functools.partial(jordan_kernel, ridge),
        in_specs=[pl.BlockSpec(memory_space=pltpu.VMEM)],
        out_specs=pl.BlockSpec(memory_space=pltpu.VMEM),
        out_shape=jax.ShapeDtypeStruct((n, 128), jnp.float32),
        scratch_shapes=[pltpu.VMEM((n, n), jnp.float32)],
        interpret=interpret,
    )(packed)[:, 0]


def ridge_solve(system, cross_sum):
    factor = jnp.linalg.cholesky(system)
    middle = lax.linalg.triangular_solve(factor, cross_sum[:, None], left_side=True, lower=True)
    answer = lax.linalg.triangular_solve(
        factor, middle, left_side=True, lower=True, transpose_a=True
    )
    return answer[:, 0]


def butterfly_sum(x, axes):
    size = 1
    for name in axes:
        size *= lax.axis_size(name)
    if size & (size - 1):
        return lax.psum(x, axes)
    step = 1
    while step < size:
        x = x + lax.ppermute(x, axes, [(i, i ^ step) for i in range(size)])
        step *= 2
    return x


def reduce_system(gram_sum, cross_sum, axes):
    n = gram_sum.shape[0]
    h = n // 2
    rows = lax.broadcasted_iota(jnp.int32, (h, h), 0)
    cols = lax.broadcasted_iota(jnp.int32, (h, h), 1)
    lead, off, trail = gram_sum[:h, :h], gram_sum[:h, h:], gram_sum[h:, h:]
    folded = jnp.where(rows <= cols, lead, trail)
    extra = jnp.stack([cross_sum, jnp.concatenate([jnp.diagonal(trail), jnp.zeros((n - h,), jnp.float32)])])
    packed = jnp.concatenate([jnp.concatenate([folded, off], 1), extra], 0)
    return butterfly_sum(packed, axes)


def local(stream, target, depthwise_taps):
    length = stream.shape[1]
    top_dilation = min(1024, length // 16)
    history_len = 15 * top_dilation + 1
    tail_end = stream[:, length - history_len :]
    previous = shifted(tail_end, ("wide", "narrow"), 1)
    span = history_len - 1
    block_len = min(TIME_BLOCK, length)
    n_blocks = length // block_len
    split = min(n_blocks, -(-span // block_len))
    window = jnp.concatenate([previous, stream], 1)[:, : split * block_len + span]
    features, gram_sum, cross_sum = features_and_sums(
        window, 0, 0, split, depthwise_taps, target, top_dilation, length
    )
    if split < n_blocks:
        delayed = jnp.concatenate([jnp.zeros_like(stream[:, :1]), stream[:, : length - 1]], 1)
        late_features, late_gram, late_cross = features_and_sums(
            delayed, span, split, n_blocks - split, depthwise_taps, target, top_dilation, length
        )
        features = (features, late_features)
        gram_sum, cross_sum = gram_sum + late_gram, cross_sum + late_cross
    else:
        features = (features,)
    cross_sum = cross_sum[0]
    packed = reduce_system(gram_sum, cross_sum, ("wide", "narrow"))
    total_rows = length * lax.axis_size("wide") * lax.axis_size("narrow")
    coefficients = ridge_solve_packed(packed, ridge_share * total_rows)
    rounded = coefficients.astype(jnp.bfloat16)
    fitted = jnp.concatenate([jnp.dot(rounded, f, preferred_element_type=jnp.float32) for f in features])
    return (coefficients, target.astype(jnp.float32) - fitted)


def solution(mesh):
    in_specs = (P(None, ("wide", "narrow")), P(("wide", "narrow")), P())
    out_specs = (P(), P(("wide", "narrow")))
    return jax.shard_map(local, mesh=mesh, in_specs=in_specs, out_specs=out_specs, check_vma=False)
```

```python
import functools

import jax
import jax.numpy as jnp
from jax import lax
from jax.sharding import PartitionSpec as P
from jax.experimental import pallas as pl
from jax.experimental.pallas import tpu as pltpu

ridge_share = 0.05


def shifted(array, axis, by):
    size = lax.axis_size(axis)
    pairs = [(i, i + by) for i in range(size) if 0 <= i + by < size]
    return lax.ppermute(array, axis, pairs)


def dilation_list(top_dilation):
    return (1, top_dilation // 16, top_dilation // 4, top_dilation)


def filter_bank(window, depthwise_taps, top_dilation, history_len, length):
    row_list = []
    for j, d in enumerate(dilation_list(top_dilation)):
        total = jnp.zeros((window.shape[0], length), jnp.float32)
        for k in range(depthwise_taps.shape[1]):
            start_offset = history_len - 1 - k * d
            total = (
                total
                + depthwise_taps[j, k][:, None] * window[:, start_offset : start_offset + length]
            )
        row_list.append(total.astype(jnp.bfloat16))
    return jnp.concatenate(row_list, 0)


TIME_BLOCK = 2048
ROW_GROUP = 16
NARROW_CHUNK = 1024
WIDE_CHUNK = 1024


def feature_kernel(dilations, span, base, first_block, taps_per_filter, w_ref, taps_ref, tgt_ref, f_ref, g_ref, c_ref):
    block = pl.program_id(0)
    block_len = f_ref.shape[1]
    channels = w_ref.shape[0]
    group = ROW_GROUP

    @pl.when(block == 0)
    def _():
        g_ref[...] = jnp.zeros_like(g_ref)
        c_ref[...] = jnp.zeros_like(c_ref)

    for j, d in enumerate(dilations):
        chunk = min(block_len, NARROW_CHUNK if d % 64 else WIDE_CHUNK)
        for g in range(channels // group):
            rows = pl.ds(g * group, group)

            def chunk_body(i, carry, j=j, d=d, rows=rows, g=g, chunk=chunk):
                start = pl.multiple_of((first_block + block) * block_len + i * chunk, 128)
                slabs = {}
                acc = None
                for k in range(taps_per_filter):
                    offset = span - k * d - base
                    r = offset % 128
                    a = offset - r
                    if r == 0:
                        x = w_ref[rows, pl.ds(pl.multiple_of(start + a, 128), chunk)].astype(jnp.float32)
                    else:
                        if a not in slabs:
                            slabs[a] = w_ref[rows, pl.ds(pl.multiple_of(start + a, 128), chunk + 128)].astype(jnp.float32)
                        x = slabs[a][:, r:r + chunk]
                    w = jnp.tile(taps_ref[j * taps_per_filter + k, rows, :], (1, chunk // 128))
                    acc = w * x if acc is None else acc + w * x
                out_rows = pl.ds(j * channels + g * group, group)
                f_ref[out_rows, pl.ds(pl.multiple_of(i * chunk, 128), chunk)] = acc.astype(f_ref.dtype)
                return carry

            lax.fori_loop(0, block_len // chunk, chunk_body, 0)

    feats = f_ref[...]
    g_ref[...] += lax.dot_general(feats, feats, (((1,), (1,)), ((), ())), preferred_element_type=jnp.float32)
    c_ref[...] += lax.dot_general(tgt_ref[...], feats, (((1,), (1,)), ((), ())), preferred_element_type=jnp.float32)


def features_and_sums(window, base, first_block, n_blocks, depthwise_taps, target, top_dilation, length, interpret=False):
    channels = window.shape[0]
    dilations = dilation_list(top_dilation)
    n_filters, taps_per_filter = len(dilations), depthwise_taps.shape[1]
    span = (taps_per_filter - 1) * top_dilation
    rows = n_filters * channels
    block_len = min(TIME_BLOCK, length)
    taps = jnp.broadcast_to(
        depthwise_taps.reshape(n_filters * taps_per_filter, channels, 1),
        (n_filters * taps_per_filter, channels, 128),
    )
    kernel = functools.partial(feature_kernel, dilations, span, base, first_block, taps_per_filter)
    return pl.pallas_call(
        kernel,
        grid=(n_blocks,),
        in_specs=[
            pl.BlockSpec(memory_space=pltpu.VMEM),
            pl.BlockSpec(memory_space=pltpu.VMEM),
            pl.BlockSpec((1, block_len), lambda b: (0, b + first_block)),
        ],
        out_specs=[
            pl.BlockSpec((rows, block_len), lambda b: (0, b)),
            pl.BlockSpec((rows, rows), lambda b: (0, 0)),
            pl.BlockSpec((1, rows), lambda b: (0, 0)),
        ],
        out_shape=[
            jax.ShapeDtypeStruct((rows, n_blocks * block_len), jnp.bfloat16),
            jax.ShapeDtypeStruct((rows, rows), jnp.float32),
            jax.ShapeDtypeStruct((1, rows), jnp.float32),
        ],
        compiler_params=pltpu.CompilerParams(
            dimension_semantics=("arbitrary",), vmem_limit_bytes=48 * 1024 * 1024
        ),
        interpret=interpret,
    )(window, taps, target.reshape(1, length))


def solve_kernel(system_ref, c_ref, x_ref, a_ref, lt_ref):
    n = a_ref.shape[0]
    a_ref[...] = system_ref[...]
    lanes = lax.broadcasted_iota(jnp.int32, (1, n), 1)
    sublanes = lax.broadcasted_iota(jnp.int32, (n, 1), 0)

    def pick(vec, at):
        return jnp.sum(jnp.where(at, vec, 0.0), axis=1, keepdims=True)

    def factor_step(j, carry):
        rhs, forward, diag = carry
        at = lanes == j
        row = a_ref[pl.ds(j, 1), :]
        root = jnp.sqrt(pick(row, at))
        col_j = jnp.where(lanes >= j, row / root, 0.0)
        lt_ref[pl.ds(j, 1), :] = col_j
        yj = pick(rhs, at) / root
        rhs = rhs - yj * col_j
        forward = jnp.where(at, yj, forward)
        diag = jnp.where(at, root, diag)
        column = jnp.sum(jnp.where(lanes == j, a_ref[...], 0.0), axis=1, keepdims=True) / root
        column = jnp.where(sublanes >= j, column, 0.0)
        a_ref[...] = a_ref[...] - column * col_j
        return rhs, forward, diag

    zeros = jnp.zeros((1, n), jnp.float32)
    _, forward, diag = lax.fori_loop(0, n, factor_step, (c_ref[...], zeros, zeros))

    def back_step(t, x):
        j = n - 1 - t
        at = lanes == j
        partial = jnp.sum(lt_ref[pl.ds(j, 1), :] * x, axis=1, keepdims=True)
        return jnp.where(at, (pick(forward, at) - partial) / pick(diag, at), x)

    x_ref[...] = lax.fori_loop(0, n, back_step, zeros)


def ridge_solve_kernel(system, cross_sum, interpret=False):
    n = system.shape[0]
    return pl.pallas_call(
        solve_kernel,
        in_specs=[pl.BlockSpec(memory_space=pltpu.VMEM), pl.BlockSpec(memory_space=pltpu.VMEM)],
        out_specs=pl.BlockSpec(memory_space=pltpu.VMEM),
        out_shape=jax.ShapeDtypeStruct((1, n), jnp.float32),
        scratch_shapes=[pltpu.VMEM((n, n), jnp.float32), pltpu.VMEM((n, n), jnp.float32)],
        interpret=interpret,
    )(system, cross_sum.reshape(1, n))[0]


def jordan_kernel(ridge, packed_ref, x_ref, a_ref):
    n = a_ref.shape[0]
    h = n // 2
    rows = lax.broadcasted_iota(jnp.int32, (h, h), 0)
    cols = lax.broadcasted_iota(jnp.int32, (h, h), 1)
    folded = packed_ref[:h, :h]
    flipped = jnp.transpose(folded)
    off = packed_ref[:h, h:]
    trail_diag = packed_ref[h + 1 : h + 2, :h]
    a_ref[:h, :h] = jnp.where(rows <= cols, folded, flipped) + jnp.where(rows == cols, ridge, 0.0)
    a_ref[:h, h:] = off
    a_ref[h:, :h] = jnp.transpose(off)
    a_ref[h:, h:] = jnp.where(rows > cols, folded, jnp.where(rows < cols, flipped, trail_diag + ridge))
    x_ref[...] = jnp.transpose(jnp.broadcast_to(packed_ref[h : h + 1, :], (128, n)))
    sublanes = lax.broadcasted_iota(jnp.int32, (n, 1), 0)

    for lo in range(0, n, 128):
        lanes = lo + lax.broadcasted_iota(jnp.int32, (1, n - lo), 1)

        def step(j, carry, lo=lo, lanes=lanes):
            at = lanes == j
            here = sublanes == j
            row = a_ref[pl.ds(j, 1), :][:, lo:]
            pivot = jnp.sum(jnp.where(at, row, 0.0), axis=1, keepdims=True)
            column = jnp.sum(jnp.where(at[:, :128], a_ref[:, lo : lo + 128], 0.0), axis=1, keepdims=True)
            scaled_row = row / pivot
            scaled_rhs = x_ref[pl.ds(j, 1), :] / pivot
            a_ref[:, lo:] = jnp.where(here, scaled_row, a_ref[:, lo:] - column * scaled_row)
            x_ref[...] = jnp.where(here, scaled_rhs, x_ref[...] - column * scaled_rhs)
            return carry

        lax.fori_loop(lo, min(n, lo + 128), step, 0)


def ridge_solve_packed(packed, ridge, interpret=False):
    n = packed.shape[1]
    return pl.pallas_call(
        functools.partial(jordan_kernel, ridge),
        in_specs=[pl.BlockSpec(memory_space=pltpu.VMEM)],
        out_specs=pl.BlockSpec(memory_space=pltpu.VMEM),
        out_shape=jax.ShapeDtypeStruct((n, 128), jnp.float32),
        scratch_shapes=[pltpu.VMEM((n, n), jnp.float32)],
        interpret=interpret,
    )(packed)[:, 0]


def ridge_solve(system, cross_sum):
    factor = jnp.linalg.cholesky(system)
    middle = lax.linalg.triangular_solve(factor, cross_sum[:, None], left_side=True, lower=True)
    answer = lax.linalg.triangular_solve(
        factor, middle, left_side=True, lower=True, transpose_a=True
    )
    return answer[:, 0]


def butterfly_sum(x, axes):
    size = 1
    for name in axes:
        size *= lax.axis_size(name)
    if size & (size - 1):
        return lax.psum(x, axes)
    step = 1
    while step < size:
        x = x + lax.ppermute(x, axes, [(i, i ^ step) for i in range(size)])
        step *= 2
    return x


def reduce_system(gram_sum, cross_sum, axes):
    n = gram_sum.shape[0]
    h = n // 2
    rows = lax.broadcasted_iota(jnp.int32, (h, h), 0)
    cols = lax.broadcasted_iota(jnp.int32, (h, h), 1)
    lead, off, trail = gram_sum[:h, :h], gram_sum[:h, h:], gram_sum[h:, h:]
    folded = jnp.where(rows <= cols, lead, trail)
    extra = jnp.stack([cross_sum, jnp.concatenate([jnp.diagonal(trail), jnp.zeros((n - h,), jnp.float32)])])
    packed = jnp.concatenate([jnp.concatenate([folded, off], 1), extra], 0)
    return butterfly_sum(packed, axes)


def local(stream, target, depthwise_taps):
    length = stream.shape[1]
    top_dilation = min(1024, length // 16)
    history_len = 15 * top_dilation + 1
    tail_end = stream[:, length - history_len :]
    previous = shifted(tail_end, ("wide", "narrow"), 1)
    span = history_len - 1
    block_len = min(TIME_BLOCK, length)
    n_blocks = length // block_len
    split = min(n_blocks, -(-span // block_len))
    window = jnp.concatenate([previous, stream], 1)[:, : split * block_len + span]
    features, gram_sum, cross_sum = features_and_sums(
        window, 0, 0, split, depthwise_taps, target, top_dilation, length
    )
    if split < n_blocks:
        delayed = jnp.concatenate([jnp.zeros_like(stream[:, :1]), stream[:, : length - 1]], 1)
        late_features, late_gram, late_cross = features_and_sums(
            delayed, span, split, n_blocks - split, depthwise_taps, target, top_dilation, length
        )
        features = (features, late_features)
        gram_sum, cross_sum = gram_sum + late_gram, cross_sum + late_cross
    else:
        features = (features,)
    cross_sum = cross_sum[0]
    packed = reduce_system(gram_sum, cross_sum, ("wide", "narrow"))
    total_rows = length * lax.axis_size("wide") * lax.axis_size("narrow")
    coefficients = ridge_solve_packed(packed, ridge_share * total_rows)
    rounded = coefficients.astype(jnp.bfloat16)
    fitted = jnp.concatenate([jnp.dot(rounded, f, preferred_element_type=jnp.float32) for f in features])
    return (coefficients, target.astype(jnp.float32) - fitted)


def solution(mesh):
    in_specs = (P(None, ("wide", "narrow")), P(("wide", "narrow")), P())
    out_specs = (P(), P(("wide", "narrow")))
    return jax.shard_map(local, mesh=mesh, in_specs=in_specs, out_specs=out_specs, check_vma=False)
```

```python
import functools

import jax
import jax.numpy as jnp
from jax import lax
from jax.sharding import PartitionSpec as P
from jax.experimental import pallas as pl
from jax.experimental.pallas import tpu as pltpu

ridge_share = 0.05


def shifted(array, axis, by):
    size = lax.axis_size(axis)
    pairs = [(i, i + by) for i in range(size) if 0 <= i + by < size]
    return lax.ppermute(array, axis, pairs)


def dilation_list(top_dilation):
    return (1, top_dilation // 16, top_dilation // 4, top_dilation)


def filter_bank(window, depthwise_taps, top_dilation, history_len, length):
    row_list = []
    for j, d in enumerate(dilation_list(top_dilation)):
        total = jnp.zeros((window.shape[0], length), jnp.float32)
        for k in range(depthwise_taps.shape[1]):
            start_offset = history_len - 1 - k * d
            total = (
                total
                + depthwise_taps[j, k][:, None] * window[:, start_offset : start_offset + length]
            )
        row_list.append(total.astype(jnp.bfloat16))
    return jnp.concatenate(row_list, 0)


TIME_BLOCK = 4096
ROW_GROUP = 16
NARROW_CHUNK = 2048
WIDE_CHUNK = 2048


def feature_kernel(dilations, span, base, first_block, taps_per_filter, w_ref, taps_ref, tgt_ref, f_ref, g_ref, c_ref):
    block = pl.program_id(0)
    block_len = f_ref.shape[1]
    channels = w_ref.shape[0]
    group = ROW_GROUP

    @pl.when(block == 0)
    def _():
        g_ref[...] = jnp.zeros_like(g_ref)
        c_ref[...] = jnp.zeros_like(c_ref)

    for j, d in enumerate(dilations):
        chunk = min(block_len, NARROW_CHUNK if d % 64 else WIDE_CHUNK)
        for g in range(channels // group):
            rows = pl.ds(g * group, group)

            def chunk_body(i, carry, j=j, d=d, rows=rows, g=g, chunk=chunk):
                start = pl.multiple_of((first_block + block) * block_len + i * chunk, 128)
                slabs = {}
                acc = None
                for k in range(taps_per_filter):
                    offset = span - k * d - base
                    r = offset % 128
                    a = offset - r
                    if r == 0:
                        x = w_ref[rows, pl.ds(pl.multiple_of(start + a, 128), chunk)].astype(jnp.float32)
                    else:
                        if a not in slabs:
                            slabs[a] = w_ref[rows, pl.ds(pl.multiple_of(start + a, 128), chunk + 128)].astype(jnp.float32)
                        x = slabs[a][:, r:r + chunk]
                    w = jnp.tile(taps_ref[j * taps_per_filter + k, rows, :], (1, chunk // 128))
                    acc = w * x if acc is None else acc + w * x
                out_rows = pl.ds(j * channels + g * group, group)
                f_ref[out_rows, pl.ds(pl.multiple_of(i * chunk, 128), chunk)] = acc.astype(f_ref.dtype)
                return carry

            lax.fori_loop(0, block_len // chunk, chunk_body, 0)

    feats = f_ref[...]
    g_ref[...] += lax.dot_general(feats, feats, (((1,), (1,)), ((), ())), preferred_element_type=jnp.float32)
    c_ref[...] += lax.dot_general(tgt_ref[...], feats, (((1,), (1,)), ((), ())), preferred_element_type=jnp.float32)


def features_and_sums(window, base, first_block, n_blocks, depthwise_taps, target, top_dilation, length, interpret=False):
    channels = window.shape[0]
    dilations = dilation_list(top_dilation)
    n_filters, taps_per_filter = len(dilations), depthwise_taps.shape[1]
    span = (taps_per_filter - 1) * top_dilation
    rows = n_filters * channels
    block_len = min(TIME_BLOCK, length)
    taps = jnp.broadcast_to(
        depthwise_taps.reshape(n_filters * taps_per_filter, channels, 1),
        (n_filters * taps_per_filter, channels, 128),
    )
    kernel = functools.partial(feature_kernel, dilations, span, base, first_block, taps_per_filter)
    return pl.pallas_call(
        kernel,
        grid=(n_blocks,),
        in_specs=[
            pl.BlockSpec(memory_space=pltpu.VMEM),
            pl.BlockSpec(memory_space=pltpu.VMEM),
            pl.BlockSpec((1, block_len), lambda b: (0, b + first_block)),
        ],
        out_specs=[
            pl.BlockSpec((rows, block_len), lambda b: (0, b)),
            pl.BlockSpec((rows, rows), lambda b: (0, 0)),
            pl.BlockSpec((1, rows), lambda b: (0, 0)),
        ],
        out_shape=[
            jax.ShapeDtypeStruct((rows, n_blocks * block_len), jnp.bfloat16),
            jax.ShapeDtypeStruct((rows, rows), jnp.float32),
            jax.ShapeDtypeStruct((1, rows), jnp.float32),
        ],
        compiler_params=pltpu.CompilerParams(
            dimension_semantics=("arbitrary",), vmem_limit_bytes=48 * 1024 * 1024
        ),
        interpret=interpret,
    )(window, taps, target.reshape(1, length))


def solve_kernel(system_ref, c_ref, x_ref, a_ref, lt_ref):
    n = a_ref.shape[0]
    a_ref[...] = system_ref[...]
    lanes = lax.broadcasted_iota(jnp.int32, (1, n), 1)
    sublanes = lax.broadcasted_iota(jnp.int32, (n, 1), 0)

    def pick(vec, at):
        return jnp.sum(jnp.where(at, vec, 0.0), axis=1, keepdims=True)

    def factor_step(j, carry):
        rhs, forward, diag = carry
        at = lanes == j
        row = a_ref[pl.ds(j, 1), :]
        root = jnp.sqrt(pick(row, at))
        col_j = jnp.where(lanes >= j, row / root, 0.0)
        lt_ref[pl.ds(j, 1), :] = col_j
        yj = pick(rhs, at) / root
        rhs = rhs - yj * col_j
        forward = jnp.where(at, yj, forward)
        diag = jnp.where(at, root, diag)
        column = jnp.sum(jnp.where(lanes == j, a_ref[...], 0.0), axis=1, keepdims=True) / root
        column = jnp.where(sublanes >= j, column, 0.0)
        a_ref[...] = a_ref[...] - column * col_j
        return rhs, forward, diag

    zeros = jnp.zeros((1, n), jnp.float32)
    _, forward, diag = lax.fori_loop(0, n, factor_step, (c_ref[...], zeros, zeros))

    def back_step(t, x):
        j = n - 1 - t
        at = lanes == j
        partial = jnp.sum(lt_ref[pl.ds(j, 1), :] * x, axis=1, keepdims=True)
        return jnp.where(at, (pick(forward, at) - partial) / pick(diag, at), x)

    x_ref[...] = lax.fori_loop(0, n, back_step, zeros)


def ridge_solve_kernel(system, cross_sum, interpret=False):
    n = system.shape[0]
    return pl.pallas_call(
        solve_kernel,
        in_specs=[pl.BlockSpec(memory_space=pltpu.VMEM), pl.BlockSpec(memory_space=pltpu.VMEM)],
        out_specs=pl.BlockSpec(memory_space=pltpu.VMEM),
        out_shape=jax.ShapeDtypeStruct((1, n), jnp.float32),
        scratch_shapes=[pltpu.VMEM((n, n), jnp.float32), pltpu.VMEM((n, n), jnp.float32)],
        interpret=interpret,
    )(system, cross_sum.reshape(1, n))[0]


def jordan_kernel(ridge, packed_ref, x_ref, a_ref):
    n = a_ref.shape[0]
    h = n // 2
    rows = lax.broadcasted_iota(jnp.int32, (h, h), 0)
    cols = lax.broadcasted_iota(jnp.int32, (h, h), 1)
    folded = packed_ref[:h, :h]
    flipped = jnp.transpose(folded)
    off = packed_ref[:h, h:]
    trail_diag = packed_ref[h + 1 : h + 2, :h]
    a_ref[:h, :h] = jnp.where(rows <= cols, folded, flipped) + jnp.where(rows == cols, ridge, 0.0)
    a_ref[:h, h:] = off
    a_ref[h:, :h] = jnp.transpose(off)
    a_ref[h:, h:] = jnp.where(rows > cols, folded, jnp.where(rows < cols, flipped, trail_diag + ridge))
    x_ref[...] = jnp.transpose(jnp.broadcast_to(packed_ref[h : h + 1, :], (128, n)))
    sublanes = lax.broadcasted_iota(jnp.int32, (n, 1), 0)

    for lo in range(0, n, 128):
        lanes = lo + lax.broadcasted_iota(jnp.int32, (1, n - lo), 1)

        def step(j, carry, lo=lo, lanes=lanes):
            at = lanes == j
            here = sublanes == j
            row = a_ref[pl.ds(j, 1), :][:, lo:]
            pivot = jnp.sum(jnp.where(at, row, 0.0), axis=1, keepdims=True)
            column = jnp.sum(jnp.where(at[:, :128], a_ref[:, lo : lo + 128], 0.0), axis=1, keepdims=True)
            scaled_row = row / pivot
            scaled_rhs = x_ref[pl.ds(j, 1), :] / pivot
            a_ref[:, lo:] = jnp.where(here, scaled_row, a_ref[:, lo:] - column * scaled_row)
            x_ref[...] = jnp.where(here, scaled_rhs, x_ref[...] - column * scaled_rhs)
            return carry

        lax.fori_loop(lo, min(n, lo + 128), step, 0)


def ridge_solve_packed(packed, ridge, interpret=False):
    n = packed.shape[1]
    return pl.pallas_call(
        functools.partial(jordan_kernel, ridge),
        in_specs=[pl.BlockSpec(memory_space=pltpu.VMEM)],
        out_specs=pl.BlockSpec(memory_space=pltpu.VMEM),
        out_shape=jax.ShapeDtypeStruct((n, 128), jnp.float32),
        scratch_shapes=[pltpu.VMEM((n, n), jnp.float32)],
        interpret=interpret,
    )(packed)[:, 0]


def ridge_solve(system, cross_sum):
    factor = jnp.linalg.cholesky(system)
    middle = lax.linalg.triangular_solve(factor, cross_sum[:, None], left_side=True, lower=True)
    answer = lax.linalg.triangular_solve(
        factor, middle, left_side=True, lower=True, transpose_a=True
    )
    return answer[:, 0]


def butterfly_sum(x, axes):
    size = 1
    for name in axes:
        size *= lax.axis_size(name)
    if size & (size - 1):
        return lax.psum(x, axes)
    step = 1
    while step < size:
        x = x + lax.ppermute(x, axes, [(i, i ^ step) for i in range(size)])
        step *= 2
    return x


def reduce_system(gram_sum, cross_sum, axes):
    n = gram_sum.shape[0]
    h = n // 2
    rows = lax.broadcasted_iota(jnp.int32, (h, h), 0)
    cols = lax.broadcasted_iota(jnp.int32, (h, h), 1)
    lead, off, trail = gram_sum[:h, :h], gram_sum[:h, h:], gram_sum[h:, h:]
    folded = jnp.where(rows <= cols, lead, trail)
    extra = jnp.stack([cross_sum, jnp.concatenate([jnp.diagonal(trail), jnp.zeros((n - h,), jnp.float32)])])
    packed = jnp.concatenate([jnp.concatenate([folded, off], 1), extra], 0)
    return butterfly_sum(packed, axes)


def local(stream, target, depthwise_taps):
    length = stream.shape[1]
    top_dilation = min(1024, length // 16)
    history_len = 15 * top_dilation + 1
    tail_end = stream[:, length - history_len :]
    previous = shifted(tail_end, ("wide", "narrow"), 1)
    span = history_len - 1
    block_len = min(TIME_BLOCK, length)
    n_blocks = length // block_len
    split = min(n_blocks, -(-span // block_len))
    window = jnp.concatenate([previous, stream], 1)[:, : split * block_len + span]
    features, gram_sum, cross_sum = features_and_sums(
        window, 0, 0, split, depthwise_taps, target, top_dilation, length
    )
    if split < n_blocks:
        delayed = jnp.concatenate([jnp.zeros_like(stream[:, :1]), stream[:, : length - 1]], 1)
        late_features, late_gram, late_cross = features_and_sums(
            delayed, span, split, n_blocks - split, depthwise_taps, target, top_dilation, length
        )
        features = (features, late_features)
        gram_sum, cross_sum = gram_sum + late_gram, cross_sum + late_cross
    else:
        features = (features,)
    cross_sum = cross_sum[0]
    packed = reduce_system(gram_sum, cross_sum, ("wide", "narrow"))
    total_rows = length * lax.axis_size("wide") * lax.axis_size("narrow")
    coefficients = ridge_solve_packed(packed, ridge_share * total_rows)
    rounded = coefficients.astype(jnp.bfloat16)
    fitted = jnp.concatenate([jnp.dot(rounded, f, preferred_element_type=jnp.float32) for f in features])
    return (coefficients, target.astype(jnp.float32) - fitted)


def solution(mesh):
    in_specs = (P(None, ("wide", "narrow")), P(("wide", "narrow")), P())
    out_specs = (P(), P(("wide", "narrow")))
    return jax.shard_map(local, mesh=mesh, in_specs=in_specs, out_specs=out_specs, check_vma=False)
```

```python
import functools

import jax
import jax.numpy as jnp
from jax import lax
from jax.sharding import PartitionSpec as P
from jax.experimental import pallas as pl
from jax.experimental.pallas import tpu as pltpu

ridge_share = 0.05


def shifted(array, axis, by):
    size = lax.axis_size(axis)
    pairs = [(i, i + by) for i in range(size) if 0 <= i + by < size]
    return lax.ppermute(array, axis, pairs)


def dilation_list(top_dilation):
    return (1, top_dilation // 16, top_dilation // 4, top_dilation)


def filter_bank(window, depthwise_taps, top_dilation, history_len, length):
    row_list = []
    for j, d in enumerate(dilation_list(top_dilation)):
        total = jnp.zeros((window.shape[0], length), jnp.float32)
        for k in range(depthwise_taps.shape[1]):
            start_offset = history_len - 1 - k * d
            total = (
                total
                + depthwise_taps[j, k][:, None] * window[:, start_offset : start_offset + length]
            )
        row_list.append(total.astype(jnp.bfloat16))
    return jnp.concatenate(row_list, 0)


TIME_BLOCK = 4096
ROW_GROUP = 16
NARROW_CHUNK = 4096
WIDE_CHUNK = 4096


def feature_kernel(dilations, span, base, first_block, taps_per_filter, w_ref, taps_ref, tgt_ref, f_ref, g_ref, c_ref):
    block = pl.program_id(0)
    block_len = f_ref.shape[1]
    channels = w_ref.shape[0]
    group = ROW_GROUP

    @pl.when(block == 0)
    def _():
        g_ref[...] = jnp.zeros_like(g_ref)
        c_ref[...] = jnp.zeros_like(c_ref)

    for j, d in enumerate(dilations):
        chunk = min(block_len, NARROW_CHUNK if d % 64 else WIDE_CHUNK)
        for g in range(channels // group):
            rows = pl.ds(g * group, group)

            def chunk_body(i, carry, j=j, d=d, rows=rows, g=g, chunk=chunk):
                start = pl.multiple_of((first_block + block) * block_len + i * chunk, 128)
                slabs = {}
                acc = None
                for k in range(taps_per_filter):
                    offset = span - k * d - base
                    r = offset % 128
                    a = offset - r
                    if r == 0:
                        x = w_ref[rows, pl.ds(pl.multiple_of(start + a, 128), chunk)].astype(jnp.float32)
                    else:
                        if a not in slabs:
                            slabs[a] = w_ref[rows, pl.ds(pl.multiple_of(start + a, 128), chunk + 128)].astype(jnp.float32)
                        x = slabs[a][:, r:r + chunk]
                    w = jnp.tile(taps_ref[j * taps_per_filter + k, rows, :], (1, chunk // 128))
                    acc = w * x if acc is None else acc + w * x
                out_rows = pl.ds(j * channels + g * group, group)
                f_ref[out_rows, pl.ds(pl.multiple_of(i * chunk, 128), chunk)] = acc.astype(f_ref.dtype)
                return carry

            lax.fori_loop(0, block_len // chunk, chunk_body, 0)

    feats = f_ref[...]
    g_ref[...] += lax.dot_general(feats, feats, (((1,), (1,)), ((), ())), preferred_element_type=jnp.float32)
    c_ref[...] += lax.dot_general(tgt_ref[...], feats, (((1,), (1,)), ((), ())), preferred_element_type=jnp.float32)


def features_and_sums(window, base, first_block, n_blocks, depthwise_taps, target, top_dilation, length, interpret=False):
    channels = window.shape[0]
    dilations = dilation_list(top_dilation)
    n_filters, taps_per_filter = len(dilations), depthwise_taps.shape[1]
    span = (taps_per_filter - 1) * top_dilation
    rows = n_filters * channels
    block_len = min(TIME_BLOCK, length)
    taps = jnp.broadcast_to(
        depthwise_taps.reshape(n_filters * taps_per_filter, channels, 1),
        (n_filters * taps_per_filter, channels, 128),
    )
    kernel = functools.partial(feature_kernel, dilations, span, base, first_block, taps_per_filter)
    return pl.pallas_call(
        kernel,
        grid=(n_blocks,),
        in_specs=[
            pl.BlockSpec(memory_space=pltpu.VMEM),
            pl.BlockSpec(memory_space=pltpu.VMEM),
            pl.BlockSpec((1, block_len), lambda b: (0, b + first_block)),
        ],
        out_specs=[
            pl.BlockSpec((rows, block_len), lambda b: (0, b)),
            pl.BlockSpec((rows, rows), lambda b: (0, 0)),
            pl.BlockSpec((1, rows), lambda b: (0, 0)),
        ],
        out_shape=[
            jax.ShapeDtypeStruct((rows, n_blocks * block_len), jnp.bfloat16),
            jax.ShapeDtypeStruct((rows, rows), jnp.float32),
            jax.ShapeDtypeStruct((1, rows), jnp.float32),
        ],
        compiler_params=pltpu.CompilerParams(
            dimension_semantics=("arbitrary",), vmem_limit_bytes=48 * 1024 * 1024
        ),
        interpret=interpret,
    )(window, taps, target.reshape(1, length))


def solve_kernel(system_ref, c_ref, x_ref, a_ref, lt_ref):
    n = a_ref.shape[0]
    a_ref[...] = system_ref[...]
    lanes = lax.broadcasted_iota(jnp.int32, (1, n), 1)
    sublanes = lax.broadcasted_iota(jnp.int32, (n, 1), 0)

    def pick(vec, at):
        return jnp.sum(jnp.where(at, vec, 0.0), axis=1, keepdims=True)

    def factor_step(j, carry):
        rhs, forward, diag = carry
        at = lanes == j
        row = a_ref[pl.ds(j, 1), :]
        root = jnp.sqrt(pick(row, at))
        col_j = jnp.where(lanes >= j, row / root, 0.0)
        lt_ref[pl.ds(j, 1), :] = col_j
        yj = pick(rhs, at) / root
        rhs = rhs - yj * col_j
        forward = jnp.where(at, yj, forward)
        diag = jnp.where(at, root, diag)
        column = jnp.sum(jnp.where(lanes == j, a_ref[...], 0.0), axis=1, keepdims=True) / root
        column = jnp.where(sublanes >= j, column, 0.0)
        a_ref[...] = a_ref[...] - column * col_j
        return rhs, forward, diag

    zeros = jnp.zeros((1, n), jnp.float32)
    _, forward, diag = lax.fori_loop(0, n, factor_step, (c_ref[...], zeros, zeros))

    def back_step(t, x):
        j = n - 1 - t
        at = lanes == j
        partial = jnp.sum(lt_ref[pl.ds(j, 1), :] * x, axis=1, keepdims=True)
        return jnp.where(at, (pick(forward, at) - partial) / pick(diag, at), x)

    x_ref[...] = lax.fori_loop(0, n, back_step, zeros)


def ridge_solve_kernel(system, cross_sum, interpret=False):
    n = system.shape[0]
    return pl.pallas_call(
        solve_kernel,
        in_specs=[pl.BlockSpec(memory_space=pltpu.VMEM), pl.BlockSpec(memory_space=pltpu.VMEM)],
        out_specs=pl.BlockSpec(memory_space=pltpu.VMEM),
        out_shape=jax.ShapeDtypeStruct((1, n), jnp.float32),
        scratch_shapes=[pltpu.VMEM((n, n), jnp.float32), pltpu.VMEM((n, n), jnp.float32)],
        interpret=interpret,
    )(system, cross_sum.reshape(1, n))[0]


def jordan_kernel(ridge, packed_ref, x_ref, a_ref):
    n = a_ref.shape[0]
    h = n // 2
    rows = lax.broadcasted_iota(jnp.int32, (h, h), 0)
    cols = lax.broadcasted_iota(jnp.int32, (h, h), 1)
    folded = packed_ref[:h, :h]
    flipped = jnp.transpose(folded)
    off = packed_ref[:h, h:]
    trail_diag = packed_ref[h + 1 : h + 2, :h]
    a_ref[:h, :h] = jnp.where(rows <= cols, folded, flipped) + jnp.where(rows == cols, ridge, 0.0)
    a_ref[:h, h:] = off
    a_ref[h:, :h] = jnp.transpose(off)
    a_ref[h:, h:] = jnp.where(rows > cols, folded, jnp.where(rows < cols, flipped, trail_diag + ridge))
    x_ref[...] = jnp.transpose(jnp.broadcast_to(packed_ref[h : h + 1, :], (128, n)))
    sublanes = lax.broadcasted_iota(jnp.int32, (n, 1), 0)

    for lo in range(0, n, 128):
        lanes = lo + lax.broadcasted_iota(jnp.int32, (1, n - lo), 1)

        def step(j, carry, lo=lo, lanes=lanes):
            at = lanes == j
            here = sublanes == j
            row = a_ref[pl.ds(j, 1), :][:, lo:]
            pivot = jnp.sum(jnp.where(at, row, 0.0), axis=1, keepdims=True)
            column = jnp.sum(jnp.where(at[:, :128], a_ref[:, lo : lo + 128], 0.0), axis=1, keepdims=True)
            scaled_row = row / pivot
            scaled_rhs = x_ref[pl.ds(j, 1), :] / pivot
            a_ref[:, lo:] = jnp.where(here, scaled_row, a_ref[:, lo:] - column * scaled_row)
            x_ref[...] = jnp.where(here, scaled_rhs, x_ref[...] - column * scaled_rhs)
            return carry

        lax.fori_loop(lo, min(n, lo + 128), step, 0)


def ridge_solve_packed(packed, ridge, interpret=False):
    n = packed.shape[1]
    return pl.pallas_call(
        functools.partial(jordan_kernel, ridge),
        in_specs=[pl.BlockSpec(memory_space=pltpu.VMEM)],
        out_specs=pl.BlockSpec(memory_space=pltpu.VMEM),
        out_shape=jax.ShapeDtypeStruct((n, 128), jnp.float32),
        scratch_shapes=[pltpu.VMEM((n, n), jnp.float32)],
        interpret=interpret,
    )(packed)[:, 0]


def ridge_solve(system, cross_sum):
    factor = jnp.linalg.cholesky(system)
    middle = lax.linalg.triangular_solve(factor, cross_sum[:, None], left_side=True, lower=True)
    answer = lax.linalg.triangular_solve(
        factor, middle, left_side=True, lower=True, transpose_a=True
    )
    return answer[:, 0]


def butterfly_sum(x, axes):
    size = 1
    for name in axes:
        size *= lax.axis_size(name)
    if size & (size - 1):
        return lax.psum(x, axes)
    step = 1
    while step < size:
        x = x + lax.ppermute(x, axes, [(i, i ^ step) for i in range(size)])
        step *= 2
    return x


def reduce_system(gram_sum, cross_sum, axes):
    n = gram_sum.shape[0]
    h = n // 2
    rows = lax.broadcasted_iota(jnp.int32, (h, h), 0)
    cols = lax.broadcasted_iota(jnp.int32, (h, h), 1)
    lead, off, trail = gram_sum[:h, :h], gram_sum[:h, h:], gram_sum[h:, h:]
    folded = jnp.where(rows <= cols, lead, trail)
    extra = jnp.stack([cross_sum, jnp.concatenate([jnp.diagonal(trail), jnp.zeros((n - h,), jnp.float32)])])
    packed = jnp.concatenate([jnp.concatenate([folded, off], 1), extra], 0)
    return butterfly_sum(packed, axes)


def local(stream, target, depthwise_taps):
    length = stream.shape[1]
    top_dilation = min(1024, length // 16)
    history_len = 15 * top_dilation + 1
    tail_end = stream[:, length - history_len :]
    previous = shifted(tail_end, ("wide", "narrow"), 1)
    span = history_len - 1
    block_len = min(TIME_BLOCK, length)
    n_blocks = length // block_len
    split = min(n_blocks, -(-span // block_len))
    window = jnp.concatenate([previous, stream], 1)[:, : split * block_len + span]
    features, gram_sum, cross_sum = features_and_sums(
        window, 0, 0, split, depthwise_taps, target, top_dilation, length
    )
    if split < n_blocks:
        delayed = jnp.concatenate([jnp.zeros_like(stream[:, :1]), stream[:, : length - 1]], 1)
        late_features, late_gram, late_cross = features_and_sums(
            delayed, span, split, n_blocks - split, depthwise_taps, target, top_dilation, length
        )
        features = (features, late_features)
        gram_sum, cross_sum = gram_sum + late_gram, cross_sum + late_cross
    else:
        features = (features,)
    cross_sum = cross_sum[0]
    packed = reduce_system(gram_sum, cross_sum, ("wide", "narrow"))
    total_rows = length * lax.axis_size("wide") * lax.axis_size("narrow")
    coefficients = ridge_solve_packed(packed, ridge_share * total_rows)
    rounded = coefficients.astype(jnp.bfloat16)
    fitted = jnp.concatenate([jnp.dot(rounded, f, preferred_element_type=jnp.float32) for f in features])
    return (coefficients, target.astype(jnp.float32) - fitted)


def solution(mesh):
    in_specs = (P(None, ("wide", "narrow")), P(("wide", "narrow")), P())
    out_specs = (P(), P(("wide", "narrow")))
    return jax.shard_map(local, mesh=mesh, in_specs=in_specs, out_specs=out_specs, check_vma=False)
```

```python
import functools

import jax
import jax.numpy as jnp
from jax import lax
from jax.sharding import PartitionSpec as P
from jax.experimental import pallas as pl
from jax.experimental.pallas import tpu as pltpu

ridge_share = 0.05


def shifted(array, axis, by):
    size = lax.axis_size(axis)
    pairs = [(i, i + by) for i in range(size) if 0 <= i + by < size]
    return lax.ppermute(array, axis, pairs)


def dilation_list(top_dilation):
    return (1, top_dilation // 16, top_dilation // 4, top_dilation)


def filter_bank(window, depthwise_taps, top_dilation, history_len, length):
    row_list = []
    for j, d in enumerate(dilation_list(top_dilation)):
        total = jnp.zeros((window.shape[0], length), jnp.float32)
        for k in range(depthwise_taps.shape[1]):
            start_offset = history_len - 1 - k * d
            total = (
                total
                + depthwise_taps[j, k][:, None] * window[:, start_offset : start_offset + length]
            )
        row_list.append(total.astype(jnp.bfloat16))
    return jnp.concatenate(row_list, 0)


TIME_BLOCK = 4096
ROW_GROUP = 16
NARROW_CHUNK = 4096
WIDE_CHUNK = 4096


def feature_kernel(dilations, span, base, first_block, taps_per_filter, w_ref, taps_ref, tgt_ref, f_ref, g_ref, c_ref, *shifted_ref):
    block = pl.program_id(0)
    block_len = f_ref.shape[1]
    channels = w_ref.shape[0]
    group = ROW_GROUP

    @pl.when(block == 0)
    def _():
        g_ref[...] = jnp.zeros_like(g_ref)
        c_ref[...] = jnp.zeros_like(c_ref)
        if shifted_ref:
            out = shifted_ref[0]
            head = w_ref[:, 0:1024].astype(jnp.float32)
            head = jnp.concatenate([jnp.zeros_like(head[:, :128]), head], 1)
            out[:, 0:1024] = head[:, 127:1151].astype(out.dtype)

            def delay(i, carry):
                at = pl.multiple_of(i * 1024, 128)
                slab = w_ref[:, pl.ds(at - 128, 1152)].astype(jnp.float32)
                out[:, pl.ds(at, 1024)] = slab[:, 127:1151].astype(out.dtype)
                return carry

            lax.fori_loop(1, w_ref.shape[1] // 1024, delay, 0)

    w_ref = shifted_ref[0] if shifted_ref else w_ref
    for j, d in enumerate(dilations):
        chunk = min(block_len, NARROW_CHUNK if d % 64 else WIDE_CHUNK)
        for g in range(channels // group):
            rows = pl.ds(g * group, group)

            def chunk_body(i, carry, j=j, d=d, rows=rows, g=g, chunk=chunk):
                start = pl.multiple_of((first_block + block) * block_len + i * chunk, 128)
                slabs = {}
                acc = None
                for k in range(taps_per_filter):
                    offset = span - k * d - base
                    r = offset % 128
                    a = offset - r
                    if r == 0:
                        x = w_ref[rows, pl.ds(pl.multiple_of(start + a, 128), chunk)].astype(jnp.float32)
                    else:
                        if a not in slabs:
                            slabs[a] = w_ref[rows, pl.ds(pl.multiple_of(start + a, 128), chunk + 128)].astype(jnp.float32)
                        x = slabs[a][:, r:r + chunk]
                    w = jnp.tile(taps_ref[j * taps_per_filter + k, rows, :], (1, chunk // 128))
                    acc = w * x if acc is None else acc + w * x
                out_rows = pl.ds(j * channels + g * group, group)
                f_ref[out_rows, pl.ds(pl.multiple_of(i * chunk, 128), chunk)] = acc.astype(f_ref.dtype)
                return carry

            lax.fori_loop(0, block_len // chunk, chunk_body, 0)

    feats = f_ref[...]
    g_ref[...] += lax.dot_general(feats, feats, (((1,), (1,)), ((), ())), preferred_element_type=jnp.float32)
    c_ref[...] += lax.dot_general(tgt_ref[...], feats, (((1,), (1,)), ((), ())), preferred_element_type=jnp.float32)


def features_and_sums(window, base, first_block, n_blocks, depthwise_taps, target, top_dilation, length, interpret=False, delay=False):
    channels = window.shape[0]
    dilations = dilation_list(top_dilation)
    n_filters, taps_per_filter = len(dilations), depthwise_taps.shape[1]
    span = (taps_per_filter - 1) * top_dilation
    rows = n_filters * channels
    block_len = min(TIME_BLOCK, length)
    taps = jnp.broadcast_to(
        depthwise_taps.reshape(n_filters * taps_per_filter, channels, 1),
        (n_filters * taps_per_filter, channels, 128),
    )
    kernel = functools.partial(feature_kernel, dilations, span, base, first_block, taps_per_filter)
    return pl.pallas_call(
        kernel,
        grid=(n_blocks,),
        in_specs=[
            pl.BlockSpec(memory_space=pltpu.VMEM),
            pl.BlockSpec(memory_space=pltpu.VMEM),
            pl.BlockSpec((1, block_len), lambda b: (0, b + first_block)),
        ],
        out_specs=[
            pl.BlockSpec((rows, block_len), lambda b: (0, b)),
            pl.BlockSpec((rows, rows), lambda b: (0, 0)),
            pl.BlockSpec((1, rows), lambda b: (0, 0)),
        ],
        out_shape=[
            jax.ShapeDtypeStruct((rows, n_blocks * block_len), jnp.bfloat16),
            jax.ShapeDtypeStruct((rows, rows), jnp.float32),
            jax.ShapeDtypeStruct((1, rows), jnp.float32),
        ],
        scratch_shapes=[pltpu.VMEM(window.shape, window.dtype)] if delay else [],
        compiler_params=pltpu.CompilerParams(
            dimension_semantics=("arbitrary",), vmem_limit_bytes=48 * 1024 * 1024
        ),
        interpret=interpret,
    )(window, taps, target.reshape(1, length))


def solve_kernel(system_ref, c_ref, x_ref, a_ref, lt_ref):
    n = a_ref.shape[0]
    a_ref[...] = system_ref[...]
    lanes = lax.broadcasted_iota(jnp.int32, (1, n), 1)
    sublanes = lax.broadcasted_iota(jnp.int32, (n, 1), 0)

    def pick(vec, at):
        return jnp.sum(jnp.where(at, vec, 0.0), axis=1, keepdims=True)

    def factor_step(j, carry):
        rhs, forward, diag = carry
        at = lanes == j
        row = a_ref[pl.ds(j, 1), :]
        root = jnp.sqrt(pick(row, at))
        col_j = jnp.where(lanes >= j, row / root, 0.0)
        lt_ref[pl.ds(j, 1), :] = col_j
        yj = pick(rhs, at) / root
        rhs = rhs - yj * col_j
        forward = jnp.where(at, yj, forward)
        diag = jnp.where(at, root, diag)
        column = jnp.sum(jnp.where(lanes == j, a_ref[...], 0.0), axis=1, keepdims=True) / root
        column = jnp.where(sublanes >= j, column, 0.0)
        a_ref[...] = a_ref[...] - column * col_j
        return rhs, forward, diag

    zeros = jnp.zeros((1, n), jnp.float32)
    _, forward, diag = lax.fori_loop(0, n, factor_step, (c_ref[...], zeros, zeros))

    def back_step(t, x):
        j = n - 1 - t
        at = lanes == j
        partial = jnp.sum(lt_ref[pl.ds(j, 1), :] * x, axis=1, keepdims=True)
        return jnp.where(at, (pick(forward, at) - partial) / pick(diag, at), x)

    x_ref[...] = lax.fori_loop(0, n, back_step, zeros)


def ridge_solve_kernel(system, cross_sum, interpret=False):
    n = system.shape[0]
    return pl.pallas_call(
        solve_kernel,
        in_specs=[pl.BlockSpec(memory_space=pltpu.VMEM), pl.BlockSpec(memory_space=pltpu.VMEM)],
        out_specs=pl.BlockSpec(memory_space=pltpu.VMEM),
        out_shape=jax.ShapeDtypeStruct((1, n), jnp.float32),
        scratch_shapes=[pltpu.VMEM((n, n), jnp.float32), pltpu.VMEM((n, n), jnp.float32)],
        interpret=interpret,
    )(system, cross_sum.reshape(1, n))[0]


def jordan_kernel(ridge, packed_ref, x_ref, a_ref):
    n = a_ref.shape[0]
    h = n // 2
    rows = lax.broadcasted_iota(jnp.int32, (h, h), 0)
    cols = lax.broadcasted_iota(jnp.int32, (h, h), 1)
    folded = packed_ref[:h, :h]
    flipped = jnp.transpose(folded)
    off = packed_ref[:h, h:]
    trail_diag = packed_ref[h + 1 : h + 2, :h]
    a_ref[:h, :h] = jnp.where(rows <= cols, folded, flipped) + jnp.where(rows == cols, ridge, 0.0)
    a_ref[:h, h:] = off
    a_ref[h:, :h] = jnp.transpose(off)
    a_ref[h:, h:] = jnp.where(rows > cols, folded, jnp.where(rows < cols, flipped, trail_diag + ridge))
    x_ref[...] = jnp.transpose(jnp.broadcast_to(packed_ref[h : h + 1, :], (128, n)))
    sublanes = lax.broadcasted_iota(jnp.int32, (n, 1), 0)

    for lo in range(0, n, 128):
        lanes = lo + lax.broadcasted_iota(jnp.int32, (1, n - lo), 1)

        def step(j, carry, lo=lo, lanes=lanes):
            at = lanes == j
            here = sublanes == j
            row = a_ref[pl.ds(j, 1), :][:, lo:]
            pivot = jnp.sum(jnp.where(at, row, 0.0), axis=1, keepdims=True)
            column = jnp.sum(jnp.where(at[:, :128], a_ref[:, lo : lo + 128], 0.0), axis=1, keepdims=True)
            scaled_row = row / pivot
            scaled_rhs = x_ref[pl.ds(j, 1), :] / pivot
            a_ref[:, lo:] = jnp.where(here, scaled_row, a_ref[:, lo:] - column * scaled_row)
            x_ref[...] = jnp.where(here, scaled_rhs, x_ref[...] - column * scaled_rhs)
            return carry

        lax.fori_loop(lo, min(n, lo + 128), step, 0)


def ridge_solve_packed(packed, ridge, interpret=False):
    n = packed.shape[1]
    return pl.pallas_call(
        functools.partial(jordan_kernel, ridge),
        in_specs=[pl.BlockSpec(memory_space=pltpu.VMEM)],
        out_specs=pl.BlockSpec(memory_space=pltpu.VMEM),
        out_shape=jax.ShapeDtypeStruct((n, 128), jnp.float32),
        scratch_shapes=[pltpu.VMEM((n, n), jnp.float32)],
        interpret=interpret,
    )(packed)[:, 0]


def ridge_solve(system, cross_sum):
    factor = jnp.linalg.cholesky(system)
    middle = lax.linalg.triangular_solve(factor, cross_sum[:, None], left_side=True, lower=True)
    answer = lax.linalg.triangular_solve(
        factor, middle, left_side=True, lower=True, transpose_a=True
    )
    return answer[:, 0]


def butterfly_sum(x, axes):
    size = 1
    for name in axes:
        size *= lax.axis_size(name)
    if size & (size - 1):
        return lax.psum(x, axes)
    step = 1
    while step < size:
        x = x + lax.ppermute(x, axes, [(i, i ^ step) for i in range(size)])
        step *= 2
    return x


def reduce_system(gram_sum, cross_sum, axes):
    n = gram_sum.shape[0]
    h = n // 2
    rows = lax.broadcasted_iota(jnp.int32, (h, h), 0)
    cols = lax.broadcasted_iota(jnp.int32, (h, h), 1)
    lead, off, trail = gram_sum[:h, :h], gram_sum[:h, h:], gram_sum[h:, h:]
    folded = jnp.where(rows <= cols, lead, trail)
    extra = jnp.stack([cross_sum, jnp.concatenate([jnp.diagonal(trail), jnp.zeros((n - h,), jnp.float32)])])
    packed = jnp.concatenate([jnp.concatenate([folded, off], 1), extra], 0)
    return butterfly_sum(packed, axes)


def local(stream, target, depthwise_taps):
    length = stream.shape[1]
    top_dilation = min(1024, length // 16)
    history_len = 15 * top_dilation + 1
    tail_end = stream[:, length - history_len :]
    previous = shifted(tail_end, ("wide", "narrow"), 1)
    span = history_len - 1
    block_len = min(TIME_BLOCK, length)
    n_blocks = length // block_len
    split = min(n_blocks, -(-span // block_len))
    window = jnp.concatenate([previous, stream], 1)[:, : split * block_len + span]
    features, gram_sum, cross_sum = features_and_sums(
        window, 0, 0, split, depthwise_taps, target, top_dilation, length
    )
    if split < n_blocks:
        late_features, late_gram, late_cross = features_and_sums(
            stream, span, split, n_blocks - split, depthwise_taps, target, top_dilation, length, delay=True
        )
        features = (features, late_features)
        gram_sum, cross_sum = gram_sum + late_gram, cross_sum + late_cross
    else:
        features = (features,)
    cross_sum = cross_sum[0]
    packed = reduce_system(gram_sum, cross_sum, ("wide", "narrow"))
    total_rows = length * lax.axis_size("wide") * lax.axis_size("narrow")
    coefficients = ridge_solve_packed(packed, ridge_share * total_rows)
    rounded = coefficients.astype(jnp.bfloat16)
    fitted = jnp.concatenate([jnp.dot(rounded, f, preferred_element_type=jnp.float32) for f in features])
    return (coefficients, target.astype(jnp.float32) - fitted)


def solution(mesh):
    in_specs = (P(None, ("wide", "narrow")), P(("wide", "narrow")), P())
    out_specs = (P(), P(("wide", "narrow")))
    return jax.shard_map(local, mesh=mesh, in_specs=in_specs, out_specs=out_specs, check_vma=False)
```
